32 devices in a mesh: seq: 8 (over z, y), mp: 4 (over x, core).
Axes of the slice: x: 2, y: 2, z: 4, core: 2. Of those that a mesh axis runs over, the one named last changes fastest.
Arguments:
- query: bfloat16 [3840, 5120], P('seq', 'mp'), may hold values from -32 to 32
- query_gain: float32 [5120], P('mp'), may hold values from 0.25 to 1.75
- cond: bfloat16 [8, 2, 128, 5120], P('seq', None, None, 'mp'), may hold values from -32 to 32
- key_gain: float32 [5120], P('mp'), may hold values from 0.25 to 1.75
- grad_out: bfloat16 [3840, 5120], P('seq', 'mp'), may hold values from -15 to 15
- clip_len: int32 [3], replicated, may hold values from 1 to 1920, 3840 in all
- clip_owner: int32 [3], replicated, may hold values from 0 to 7, as said below
Outputs:
- grad_query: bfloat16 [3840, 5120], P('seq', 'mp')
- grad_cond: bfloat16 [8, 2, 128, 5120], P('seq', None, None, 'mp')
The draws below stay inside these ranges and needn't reach their ends.
Inputs may be any that keep to these rules, and one draw needn't show every extreme that they name: `clip_len`: the clip lengths sum to 3840, and the longest is exactly 1920. `clip_owner`: the owners of the 3 clips are distinct slots.
All inputs are finite; a program needn't handle non-finite values.
Results may differ from the reference program's by a relative error of at most 0.011.
Values may be sent and summed in bfloat16 or wider, within the bound.
No kernel may reach another device: no remote copies, remote signals or barrier semaphores. Data moves between devices by JAX's collectives and lax.ppermute only.
A program may use at most 128 MiB of HBM per device.

```python
import math
import jax
import jax.numpy as jnp
import numpy as np
from jax import lax

D = 5120
HEADS = 40
HEAD_DIM = 128
ROWS = 128
CLIPS = 3
TOKENS = 3840
SLOTS = 8


def column_profile(key, count, rising):
    spread = jnp.exp(jax.random.uniform(key, (count,), minval=0.0, maxval=math.log(10.0)))
    ramp = 1.0 + (rising - 1.0) * jnp.arange(count, dtype=jnp.float32) / (count - 1)
    return spread * ramp / 10.0


def draw_query(key, part):
    base = jax.random.fold_in(key, 11)
    noise_key, row_key, col_key = jax.random.split(base, 3)
    noise = jax.random.normal(noise_key, (TOKENS, D))
    columns = column_profile(col_key, D, 3.0)
    row_scales = jnp.exp(jax.random.uniform(row_key, (TOKENS, 1), minval=math.log(0.3), maxval=math.log(3.0)))
    value = noise * row_scales * columns[None, :]
    return jnp.clip(value, -32.0, 32.0).astype(jnp.bfloat16)


def draw_cond(key, part):
    base = jax.random.fold_in(key, 22)
    noise_key, row_key, col_key, value_key = jax.random.split(base, 4)
    noise = jax.random.normal(noise_key, (SLOTS, ROWS, D))
    columns = column_profile(col_key, D, 3.0)
    value_part = jax.random.normal(value_key, (SLOTS, ROWS, D))
    row_scales = jnp.exp(jax.random.uniform(row_key, (SLOTS, ROWS, 1), minval=math.log(0.3), maxval=math.log(3.0)))
    key_part = noise * row_scales * columns[None, None, :]
    stacked = jnp.stack([key_part, value_part], axis=1)
    return jnp.clip(stacked, -32.0, 32.0).astype(jnp.bfloat16)


def draw_clip_owner(key, part):
    base = jax.random.fold_in(key, 33)
    pick_key, order_key = jax.random.split(base, 2)
    middle = jax.random.permutation(pick_key, jnp.arange(SLOTS - 2, dtype=jnp.int32))[:CLIPS - 2] + 1
    ends = jnp.array([0, SLOTS - 1], dtype=jnp.int32)
    combined = jnp.concatenate([middle.astype(jnp.int32), ends])
    return jax.random.permutation(order_key, combined).astype(jnp.int32)


def levels(own_key, extent, shards, low, high):
    factor_of = 1.0
    for dim, shards_of in shards:
        heights = jax.random.uniform(jax.random.fold_in(jax.random.fold_in(own_key, 6), dim), (shards_of,), jnp.float32, low / len(shards), high / len(shards))
        factor_of = factor_of * jnp.repeat(jnp.exp(heights), extent[dim] // shards_of).reshape((-1,) + (1,) * (len(extent) - 1 - dim))
    return factor_of


def split_up(amount, total, bound, slope):
    loads = [(1 << 20) // math.isqrt(rank ** slope) + 1 for rank in range(2, amount + 1)]
    rest, counts = total - bound - (amount - 1), [1] * (amount - 1)
    while rest > 0:
        free = [i for i in range(amount - 1) if counts[i] < bound]
        pool, budget = sum([loads[i] for i in free]), rest
        for i in free:
            more = min(bound - counts[i], max(1, budget * loads[i] // pool), rest)
            counts[i] = counts[i] + more
            rest = rest - more
    return np.array([bound] + counts)


def uneven(rng, count, total, reach, slope):
    if count == 2:
        one = jax.random.randint(rng, (), max(1, total - reach), min(reach, total - 1) + 1)
        return jnp.stack([one, total - one])
    sizes = jnp.asarray(split_up(count, total, reach, slope), jnp.int32)
    pairs = (count - 1) // 2
    donor, sink = sizes[1:1 + 2 * pairs:2], sizes[2:2 + 2 * pairs:2]
    margin = jnp.minimum(donor - 1, reach - sink)
    moved = jax.random.randint(jax.random.fold_in(rng, 1), (pairs,), 0, 1 << 20) % (margin + 1)
    sizes = sizes.at[1:1 + 2 * pairs:2].set(donor - moved).at[2:2 + 2 * pairs:2].set(sink + moved)
    return sizes[jax.random.permutation(jax.random.fold_in(rng, 2), count)]


def normal_values(stream_key, shape, width, bound, pieces=(), held_as=jnp.bfloat16):
    values = width * jax.random.normal(stream_key, shape, jnp.float32)
    if pieces:
        values = values * levels(stream_key, shape, pieces, -0.22, 0.18)
    return jnp.clip(values, -bound, bound).astype(held_as)


def setup_inputs(seed: int = 0) -> dict:
    streams_of = jax.random.split(jax.random.key(seed), 8)
    query = draw_query(jax.random.fold_in(streams_of[7], 71), 0)
    query_gain = jnp.clip(1.0 + 0.15 * jax.random.normal(streams_of[1], (D,), jnp.float32), 0.25, 1.75)
    cond = draw_cond(jax.random.fold_in(streams_of[7], 71), 0)
    key_gain = jnp.clip(1.0 + 0.15 * jax.random.normal(streams_of[3], (D,), jnp.float32), 0.25, 1.75)
    grad_out = normal_values(streams_of[4], (TOKENS, D), 2.5, 15.0, ((0, 8), (1, 4)))
    clip_len = uneven(streams_of[5], CLIPS, TOKENS, TOKENS // 2, 2).astype(jnp.int32)
    clip_owner = draw_clip_owner(jax.random.fold_in(streams_of[7], 71), 0)
    return {"query": query, "query_gain": query_gain, "cond": cond, "key_gain": key_gain, "grad_out": grad_out, "clip_len": clip_len, "clip_owner": clip_owner}


EPS = 1e-06
MASKED = -1e+30

def reference(query, query_gain, cond, key_gain, grad_out, clip_len, clip_owner):
    starts = (jnp.cumsum(clip_len) - clip_len).astype(jnp.int32)
    position = jnp.arange(TOKENS, dtype=jnp.int32)
    clip_of = lax.optimization_barrier(jnp.sum((position[:, None] >= starts[None, :]).astype(jnp.int32), axis=1)) - 1
    query_wide = query.astype(jnp.float32)
    query_scale = lax.rsqrt(lax.optimization_barrier(jnp.sum(query_wide * query_wide, axis=1)) / D + EPS)
    query_normed = (query_wide * query_scale[:, None] * query_gain).astype(jnp.bfloat16)
    slab_stack = cond[clip_owner]
    key_raw = slab_stack[:, 0].astype(jnp.float32)
    key_scale = lax.rsqrt(lax.optimization_barrier(jnp.sum(key_raw * key_raw, axis=2)) / D + EPS)
    key_normed = (key_raw * key_scale[:, :, None] * key_gain).astype(jnp.bfloat16).reshape(CLIPS * ROWS, D)
    value_rows = slab_stack[:, 1].reshape(CLIPS * ROWS, D)
    key_clip = jnp.arange(CLIPS * ROWS, dtype=jnp.int32) // ROWS
    allowed = clip_of[:, None] == key_clip[None, :]
    score_scale = 1.0 / math.sqrt(HEAD_DIM)

    def one_head(head):
        start = head * HEAD_DIM
        query_head = lax.dynamic_slice_in_dim(query_normed, start, HEAD_DIM, 1)
        key_head = lax.dynamic_slice_in_dim(key_normed, start, HEAD_DIM, 1)
        value_head = lax.dynamic_slice_in_dim(value_rows, start, HEAD_DIM, 1)
        grad_head = lax.dynamic_slice_in_dim(grad_out, start, HEAD_DIM, 1)
        scores = jnp.dot(query_head, key_head.T, preferred_element_type=jnp.float32) * score_scale
        scores = jnp.where(allowed, scores, MASKED)
        row_max = lax.optimization_barrier(jnp.max(scores, axis=1, keepdims=True))
        weights = jnp.exp(scores - row_max)
        normed_weights = weights / lax.optimization_barrier(jnp.sum(weights, axis=1, keepdims=True))
        weights_low = normed_weights.astype(jnp.bfloat16)
        attended = jnp.dot(weights_low, value_head, preferred_element_type=jnp.float32).astype(jnp.bfloat16)
        delta = lax.optimization_barrier(jnp.sum(grad_head.astype(jnp.float32) * attended.astype(jnp.float32), axis=1))
        grad_weights = jnp.dot(grad_head, value_head.T, preferred_element_type=jnp.float32)
        grad_scores = (normed_weights * (grad_weights - delta[:, None]) * score_scale).astype(jnp.bfloat16)
        grad_q = jnp.dot(grad_scores, key_head, preferred_element_type=jnp.float32)
        grad_k = jnp.dot(grad_scores.T, query_head, preferred_element_type=jnp.float32)
        grad_v = jnp.dot(weights_low.T, grad_head, preferred_element_type=jnp.float32)
        return (grad_q, grad_k, grad_v)
    grad_q, grad_k, grad_v = lax.map(one_head, jnp.arange(HEADS, dtype=jnp.int32))
    grad_query = jnp.transpose(grad_q, (1, 0, 2)).reshape(TOKENS, D).astype(jnp.bfloat16)
    key_grad = jnp.transpose(grad_k, (1, 0, 2)).reshape(CLIPS, ROWS, D)
    value_grad = jnp.transpose(grad_v, (1, 0, 2)).reshape(CLIPS, ROWS, D)
    stacked = jnp.stack([key_grad, value_grad], axis=1).astype(jnp.bfloat16)
    grad_cond = jnp.zeros((SLOTS, 2, ROWS, D), jnp.bfloat16).at[clip_owner].set(stacked)
    return (grad_query, grad_cond)
```

```python
import math

import jax
import jax.numpy as jnp
from jax import lax
from jax.experimental import pallas as pl
from jax.experimental.pallas import tpu as pltpu
from jax.sharding import PartitionSpec as P

D = 5120
HEAD_DIM = 128


EPS = 1e-06
MASKED = -1e30


def attend_kernel(tok_clip_ref, key_clip_ref, q_ref, k_ref, v_ref, g_ref, dq_ref, dk_ref, dv_ref):
    score_scale = 1.0 / math.sqrt(HEAD_DIM)
    q = q_ref[...]
    k = k_ref[...]
    v = v_ref[...]
    g = g_ref[...]
    allowed = tok_clip_ref[...] == key_clip_ref[...]
    nt = (((1,), (1,)), ((), ()))
    tn = (((0,), (0,)), ((), ()))
    scores = lax.dot_general(q, k, nt, preferred_element_type=jnp.float32) * score_scale
    scores = jnp.where(allowed, scores, MASKED)
    row_max = jnp.max(scores, axis=1, keepdims=True)
    weights = jnp.exp(scores - row_max)
    normed = weights / jnp.sum(weights, axis=1, keepdims=True)
    weights_low = normed.astype(jnp.bfloat16)
    attended = jnp.dot(weights_low, v, preferred_element_type=jnp.float32).astype(jnp.bfloat16)
    delta = jnp.sum(g.astype(jnp.float32) * attended.astype(jnp.float32), axis=1, keepdims=True)
    grad_weights = lax.dot_general(g, v, nt, preferred_element_type=jnp.float32)
    grad_scores = (normed * (grad_weights - delta) * score_scale).astype(jnp.bfloat16)
    dq_ref[...] = jnp.dot(grad_scores, k, preferred_element_type=jnp.float32).astype(dq_ref.dtype)
    dk_ref[...] = lax.dot_general(grad_scores, q, tn, preferred_element_type=jnp.float32)
    dv_ref[...] = lax.dot_general(weights_low, g, tn, preferred_element_type=jnp.float32)


def attend(tok_clip, key_clip, query_normed, keys, values, grad_out):
    tok_rows, feat_width = query_normed.shape
    key_rows = keys.shape[0]
    head_count = feat_width // HEAD_DIM
    tok_spec = pl.BlockSpec((tok_rows, HEAD_DIM), lambda h: (0, h))
    key_spec = pl.BlockSpec((key_rows, HEAD_DIM), lambda h: (0, h))
    return pl.pallas_call(
        attend_kernel,
        grid=(head_count,),
        in_specs=[
            pl.BlockSpec((tok_rows, 1), lambda h: (0, 0)),
            pl.BlockSpec((1, key_rows), lambda h: (0, 0)),
            tok_spec,
            key_spec,
            key_spec,
            tok_spec,
        ],
        out_specs=[tok_spec, key_spec, key_spec],
        out_shape=[
            jax.ShapeDtypeStruct((tok_rows, feat_width), jnp.bfloat16),
            jax.ShapeDtypeStruct((key_rows, feat_width), jnp.float32),
            jax.ShapeDtypeStruct((key_rows, feat_width), jnp.float32),
        ],
        compiler_params=pltpu.CompilerParams(dimension_semantics=("arbitrary",)),
    )(tok_clip, key_clip, query_normed, keys, values, grad_out)


def local(query, query_gain, cond, key_gain, grad_out, clip_len, clip_owner):
    tok_rows = query.shape[0]
    clip_count = clip_len.shape[0]
    cond_depth = cond.shape[2]
    my_index = lax.axis_index("seq")
    first_pos = my_index * tok_rows
    position = first_pos + jnp.arange(tok_rows, dtype=jnp.int32)
    starts = jnp.cumsum(clip_len) - clip_len
    clip_of = jnp.sum((position[:, None] >= starts[None, :]).astype(jnp.int32), axis=1) - 1
    query_wide = query.astype(jnp.float32)
    own_key = cond[0, 0].astype(jnp.float32)
    sums = lax.psum(
        (jnp.sum(query_wide * query_wide, axis=1), jnp.sum(own_key * own_key, axis=1)), "mp"
    )
    query_scale = lax.rsqrt(sums[0] / D + EPS)
    query_normed = (query_wide * query_scale[:, None] * query_gain).astype(jnp.bfloat16)
    key_scale = lax.rsqrt(sums[1] / D + EPS)
    own_key_normed = (own_key * key_scale[:, None] * key_gain).astype(jnp.bfloat16)
    own_slab = jnp.stack([own_key_normed, cond[0, 1]])
    owned = clip_owner == my_index
    slabs = lax.psum(
        jnp.where(owned[:, None, None, None], own_slab[None], jnp.zeros_like(own_slab)[None]),
        "seq",
    )
    first_clip = clip_of[0]
    second_clip = first_clip + 1
    second_index = jnp.minimum(second_clip, clip_count - 1)
    slab_a = lax.dynamic_index_in_dim(slabs, first_clip, 0, keepdims=False)
    slab_b = lax.dynamic_index_in_dim(slabs, second_index, 0, keepdims=False)
    keys = jnp.concatenate([slab_a[0], slab_b[0]], axis=0)
    values = jnp.concatenate([slab_a[1], slab_b[1]], axis=0)
    key_clip = jnp.concatenate(
        [jnp.full((cond_depth,), first_clip, jnp.int32), jnp.full((cond_depth,), second_clip, jnp.int32)]
    )
    grad_query, key_grad, value_grad = attend(
        clip_of[:, None], key_clip[None, :], query_normed, keys, values, grad_out
    )
    part_a = jnp.stack([key_grad[:cond_depth], value_grad[:cond_depth]])
    part_b = jnp.stack([key_grad[cond_depth:], value_grad[cond_depth:]])
    clip_ids = jnp.arange(clip_count, dtype=jnp.int32)[:, None, None, None]
    partial_grads = jnp.where(clip_ids == first_clip, part_a[None], 0.0) + jnp.where(
        clip_ids == second_clip, part_b[None], 0.0
    )
    summed = lax.psum(partial_grads, "seq")
    my_clip = jnp.sum(jnp.where(owned, jnp.arange(clip_count, dtype=jnp.int32), 0))
    mine = lax.dynamic_index_in_dim(summed, my_clip, 0, keepdims=False)
    owned_grads = jnp.where(jnp.any(owned), mine, 0.0).astype(jnp.bfloat16)
    return (grad_query, owned_grads[None])


def solution(mesh):
    return jax.shard_map(
        local,
        mesh=mesh,
        in_specs=(
            P("seq", "mp"),
            P("mp"),
            P("seq", None, None, "mp"),
            P("mp"),
            P("seq", "mp"),
            P(),
            P(),
        ),
        out_specs=(P("seq", "mp"), P("seq", None, None, "mp")),
        check_vma=False,
    )
```

```python
import math

import jax
import jax.numpy as jnp
from jax import lax
from jax.experimental import pallas as pl
from jax.experimental.pallas import tpu as pltpu
from jax.sharding import PartitionSpec as P

D = 5120
HEAD_DIM = 128


EPS = 1e-06
MASKED = -1e30


def attend_kernel(tok_clip_ref, key_clip_ref, q_ref, k_ref, v_ref, g_ref, dq_ref, dk_ref, dv_ref):
    score_scale = 1.0 / math.sqrt(HEAD_DIM)
    q = q_ref[...]
    k = k_ref[...]
    v = v_ref[...]
    g = g_ref[...]
    allowed = tok_clip_ref[...] == key_clip_ref[...]
    nt = (((1,), (1,)), ((), ()))
    tn = (((0,), (0,)), ((), ()))
    scores = lax.dot_general(q, k, nt, preferred_element_type=jnp.float32) * score_scale
    scores = jnp.where(allowed, scores, MASKED)
    row_max = jnp.max(scores, axis=1, keepdims=True)
    weights = jnp.exp(scores - row_max)
    normed = weights / jnp.sum(weights, axis=1, keepdims=True)
    weights_low = normed.astype(jnp.bfloat16)
    attended = jnp.dot(weights_low, v, preferred_element_type=jnp.float32).astype(jnp.bfloat16)
    delta = jnp.sum(g.astype(jnp.float32) * attended.astype(jnp.float32), axis=1, keepdims=True)
    grad_weights = lax.dot_general(g, v, nt, preferred_element_type=jnp.float32)
    grad_scores = (normed * (grad_weights - delta) * score_scale).astype(jnp.bfloat16)
    dq_ref[...] = jnp.dot(grad_scores, k, preferred_element_type=jnp.float32).astype(dq_ref.dtype)
    dk_ref[...] = lax.dot_general(grad_scores, q, tn, preferred_element_type=jnp.float32)
    dv_ref[...] = lax.dot_general(weights_low, g, tn, preferred_element_type=jnp.float32)


def attend(tok_clip, key_clip, query_normed, keys, values, grad_out):
    tok_rows, feat_width = query_normed.shape
    key_rows = keys.shape[0]
    head_count = feat_width // HEAD_DIM
    tok_spec = pl.BlockSpec((tok_rows, HEAD_DIM), lambda h: (0, h))
    key_spec = pl.BlockSpec((key_rows, HEAD_DIM), lambda h: (0, h))
    return pl.pallas_call(
        attend_kernel,
        grid=(head_count,),
        in_specs=[
            pl.BlockSpec((tok_rows, 1), lambda h: (0, 0)),
            pl.BlockSpec((1, key_rows), lambda h: (0, 0)),
            tok_spec,
            key_spec,
            key_spec,
            tok_spec,
        ],
        out_specs=[tok_spec, key_spec, key_spec],
        out_shape=[
            jax.ShapeDtypeStruct((tok_rows, feat_width), jnp.bfloat16),
            jax.ShapeDtypeStruct((key_rows, feat_width), jnp.float32),
            jax.ShapeDtypeStruct((key_rows, feat_width), jnp.float32),
        ],
        compiler_params=pltpu.CompilerParams(dimension_semantics=("arbitrary",)),
    )(tok_clip, key_clip, query_normed, keys, values, grad_out)


def local(query, query_gain, cond, key_gain, grad_out, clip_len, clip_owner, seq_count):
    tok_rows, feat_width = query.shape
    clip_count = clip_len.shape[0]
    cond_depth = cond.shape[2]
    piece = cond_depth // seq_count
    my_index = lax.axis_index("seq")
    first_pos = my_index * tok_rows
    position = first_pos + jnp.arange(tok_rows, dtype=jnp.int32)
    starts = jnp.cumsum(clip_len) - clip_len
    clip_of = jnp.sum((position[:, None] >= starts[None, :]).astype(jnp.int32), axis=1) - 1
    device_pos = jnp.arange(seq_count, dtype=jnp.int32) * tok_rows
    device_first = jnp.sum((device_pos[:, None] >= starts[None, :]).astype(jnp.int32), axis=1) - 1
    query_wide = query.astype(jnp.float32)
    own_key = cond[0, 0].astype(jnp.float32)
    sums = lax.psum(
        (jnp.sum(query_wide * query_wide, axis=1), jnp.sum(own_key * own_key, axis=1)), "mp"
    )
    query_scale = lax.rsqrt(sums[0] / D + EPS)
    query_normed = (query_wide * query_scale[:, None] * query_gain).astype(jnp.bfloat16)
    key_scale = lax.rsqrt(sums[1] / D + EPS)
    own_key_normed = (own_key * key_scale[:, None] * key_gain).astype(jnp.bfloat16)
    own_slab = jnp.stack([own_key_normed, cond[0, 1]])
    spread = own_slab.reshape(2, seq_count, piece, feat_width).transpose(1, 0, 2, 3)
    gathered = lax.all_to_all(spread, "seq", 0, 0, tiled=True)
    clip_rows = jnp.take(gathered, clip_owner, axis=0)
    slot_clip = jnp.stack([device_first, device_first + 1], axis=1)
    wanted = jnp.take(clip_rows, jnp.minimum(slot_clip, clip_count - 1), axis=0)
    arrived = lax.all_to_all(wanted, "seq", 0, 0, tiled=True)
    mine = arrived.transpose(1, 2, 0, 3, 4).reshape(2, 2, cond_depth, feat_width)
    keys = mine[:, 0].reshape(2 * cond_depth, feat_width)
    values = mine[:, 1].reshape(2 * cond_depth, feat_width)
    first_clip = device_first[my_index]
    key_clip = jnp.concatenate(
        [jnp.full((cond_depth,), first_clip, jnp.int32), jnp.full((cond_depth,), first_clip + 1, jnp.int32)]
    )
    grad_query, key_grad, value_grad = attend(
        clip_of[:, None], key_clip[None, :], query_normed, keys, values, grad_out
    )
    partial = jnp.stack(
        [key_grad.reshape(2, cond_depth, feat_width), value_grad.reshape(2, cond_depth, feat_width)], axis=1
    ).astype(jnp.bfloat16)
    spread_grads = partial.reshape(2, 2, seq_count, piece, feat_width).transpose(2, 0, 1, 3, 4)
    pieces = lax.all_to_all(spread_grads, "seq", 0, 0, tiled=True)
    source_clip = slot_clip.reshape(2 * seq_count)
    onehot = (source_clip[:, None] == jnp.arange(clip_count, dtype=jnp.int32)[None, :]).astype(jnp.bfloat16)
    summed = jnp.einsum(
        "sc,sx->cx", onehot, pieces.reshape(2 * seq_count, -1), preferred_element_type=jnp.float32
    ).astype(jnp.bfloat16).reshape(clip_count, 2, piece, feat_width)
    owns = clip_owner[None, :] == jnp.arange(seq_count, dtype=jnp.int32)[:, None]
    owned_clip = jnp.sum(jnp.where(owns, jnp.arange(clip_count, dtype=jnp.int32)[None, :], 0), axis=1)
    outgoing = jnp.where(
        jnp.any(owns, axis=1)[:, None, None, None], jnp.take(summed, owned_clip, axis=0), jnp.zeros((), jnp.bfloat16)
    )
    returned = lax.all_to_all(outgoing, "seq", 0, 0, tiled=True)
    owned_grads = returned.transpose(1, 0, 2, 3).reshape(2, cond_depth, feat_width)
    return (grad_query, owned_grads[None])


def solution(mesh):
    seq_count = mesh.shape["seq"]

    def body(*args):
        return local(*args, seq_count)

    return jax.shard_map(
        body,
        mesh=mesh,
        in_specs=(
            P("seq", "mp"),
            P("mp"),
            P("seq", None, None, "mp"),
            P("mp"),
            P("seq", "mp"),
            P(),
            P(),
        ),
        out_specs=(P("seq", "mp"), P("seq", None, None, "mp")),
        check_vma=False,
    )
```

```python
import math

import jax
import jax.numpy as jnp
from jax import lax
from jax.experimental import pallas as pl
from jax.experimental.pallas import tpu as pltpu
from jax.sharding import PartitionSpec as P

D = 5120
HEAD_DIM = 128


EPS = 1e-06
MASKED = -1e30


HEADS_PER_STEP = 2


def attend_kernel(tok_clip_ref, key_clip_ref, q_ref, k_ref, v_ref, g_ref, dq_ref, dk_ref, dv_ref):
    score_scale = 1.0 / math.sqrt(HEAD_DIM)
    allowed = tok_clip_ref[...] == key_clip_ref[...]
    nt = (((1,), (1,)), ((), ()))
    tn = (((0,), (0,)), ((), ()))
    for head in range(HEADS_PER_STEP):
        cols = slice(head * HEAD_DIM, (head + 1) * HEAD_DIM)
        q = q_ref[:, cols]
        k = k_ref[:, cols]
        v = v_ref[:, cols]
        g = g_ref[:, cols]
        scores = lax.dot_general(q, k, nt, preferred_element_type=jnp.float32) * score_scale
        scores = jnp.where(allowed, scores, MASKED)
        row_max = jnp.max(scores, axis=1, keepdims=True)
        weights = jnp.exp(scores - row_max)
        normed = weights * (1.0 / jnp.sum(weights, axis=1, keepdims=True))
        weights_low = normed.astype(jnp.bfloat16)
        attended = jnp.dot(weights_low, v, preferred_element_type=jnp.float32).astype(jnp.bfloat16)
        delta = jnp.sum(g.astype(jnp.float32) * attended.astype(jnp.float32), axis=1, keepdims=True)
        grad_weights = lax.dot_general(g, v, nt, preferred_element_type=jnp.float32)
        grad_scores = (normed * (grad_weights - delta) * score_scale).astype(jnp.bfloat16)
        dq_ref[:, cols] = jnp.dot(grad_scores, k, preferred_element_type=jnp.float32).astype(dq_ref.dtype)
        dk_ref[:, cols] = lax.dot_general(grad_scores, q, tn, preferred_element_type=jnp.float32)
        dv_ref[:, cols] = lax.dot_general(weights_low, g, tn, preferred_element_type=jnp.float32)


def attend(tok_clip, key_clip, query_normed, keys, values, grad_out):
    tok_rows, feat_width = query_normed.shape
    key_rows = keys.shape[0]
    step_width = HEADS_PER_STEP * HEAD_DIM
    tok_spec = pl.BlockSpec((tok_rows, step_width), lambda h: (0, h))
    key_spec = pl.BlockSpec((key_rows, step_width), lambda h: (0, h))
    return pl.pallas_call(
        attend_kernel,
        grid=(feat_width // step_width,),
        in_specs=[
            pl.BlockSpec((tok_rows, 1), lambda h: (0, 0)),
            pl.BlockSpec((1, key_rows), lambda h: (0, 0)),
            tok_spec,
            key_spec,
            key_spec,
            tok_spec,
        ],
        out_specs=[tok_spec, key_spec, key_spec],
        out_shape=[
            jax.ShapeDtypeStruct((tok_rows, feat_width), jnp.bfloat16),
            jax.ShapeDtypeStruct((key_rows, feat_width), jnp.float32),
            jax.ShapeDtypeStruct((key_rows, feat_width), jnp.float32),
        ],
        compiler_params=pltpu.CompilerParams(dimension_semantics=("arbitrary",)),
    )(tok_clip, key_clip, query_normed, keys, values, grad_out)


def local(query, query_gain, cond, key_gain, grad_out, clip_len, clip_owner, seq_count):
    tok_rows, feat_width = query.shape
    clip_count = clip_len.shape[0]
    cond_depth = cond.shape[2]
    piece = cond_depth // seq_count
    my_index = lax.axis_index("seq")
    first_pos = my_index * tok_rows
    position = first_pos + jnp.arange(tok_rows, dtype=jnp.int32)
    starts = jnp.cumsum(clip_len) - clip_len
    clip_of = jnp.sum((position[:, None] >= starts[None, :]).astype(jnp.int32), axis=1) - 1
    device_pos = jnp.arange(seq_count, dtype=jnp.int32) * tok_rows
    device_first = jnp.sum((device_pos[:, None] >= starts[None, :]).astype(jnp.int32), axis=1) - 1
    query_wide = query.astype(jnp.float32)
    own_key = cond[0, 0].astype(jnp.float32)
    sums = lax.psum(
        (jnp.sum(query_wide * query_wide, axis=1), jnp.sum(own_key * own_key, axis=1)), "mp"
    )
    query_scale = lax.rsqrt(sums[0] / D + EPS)
    query_normed = (query_wide * query_scale[:, None] * query_gain).astype(jnp.bfloat16)
    key_scale = lax.rsqrt(sums[1] / D + EPS)
    own_key_normed = (own_key * key_scale[:, None] * key_gain).astype(jnp.bfloat16)
    own_slab = jnp.stack([own_key_normed, cond[0, 1]])
    spread = own_slab.reshape(2, seq_count, piece, feat_width).transpose(1, 0, 2, 3)
    gathered = lax.all_to_all(spread, "seq", 0, 0, tiled=True)
    clip_rows = jnp.take(gathered, clip_owner, axis=0)
    slot_clip = jnp.stack([device_first, device_first + 1], axis=1)
    wanted = jnp.take(clip_rows, jnp.minimum(slot_clip, clip_count - 1), axis=0)
    arrived = lax.all_to_all(wanted, "seq", 0, 0, tiled=True)
    mine = arrived.transpose(1, 2, 0, 3, 4).reshape(2, 2, cond_depth, feat_width)
    keys = mine[:, 0].reshape(2 * cond_depth, feat_width)
    values = mine[:, 1].reshape(2 * cond_depth, feat_width)
    first_clip = device_first[my_index]
    key_clip = jnp.concatenate(
        [jnp.full((cond_depth,), first_clip, jnp.int32), jnp.full((cond_depth,), first_clip + 1, jnp.int32)]
    )
    grad_query, key_grad, value_grad = attend(
        clip_of[:, None], key_clip[None, :], query_normed, keys, values, grad_out
    )
    partial = jnp.stack(
        [key_grad.reshape(2, cond_depth, feat_width), value_grad.reshape(2, cond_depth, feat_width)], axis=1
    ).astype(jnp.bfloat16)
    spread_grads = partial.reshape(2, 2, seq_count, piece, feat_width).transpose(2, 0, 1, 3, 4)
    pieces = lax.all_to_all(spread_grads, "seq", 0, 0, tiled=True)
    source_clip = slot_clip.reshape(2 * seq_count)
    onehot = (source_clip[:, None] == jnp.arange(clip_count, dtype=jnp.int32)[None, :]).astype(jnp.bfloat16)
    summed = jnp.einsum(
        "sc,sx->cx", onehot, pieces.reshape(2 * seq_count, -1), preferred_element_type=jnp.float32
    ).astype(jnp.bfloat16).reshape(clip_count, 2, piece, feat_width)
    owns = clip_owner[None, :] == jnp.arange(seq_count, dtype=jnp.int32)[:, None]
    owned_clip = jnp.sum(jnp.where(owns, jnp.arange(clip_count, dtype=jnp.int32)[None, :], 0), axis=1)
    outgoing = jnp.where(
        jnp.any(owns, axis=1)[:, None, None, None], jnp.take(summed, owned_clip, axis=0), jnp.zeros((), jnp.bfloat16)
    )
    returned = lax.all_to_all(outgoing, "seq", 0, 0, tiled=True)
    owned_grads = returned.transpose(1, 0, 2, 3).reshape(2, cond_depth, feat_width)
    return (grad_query, owned_grads[None])


def solution(mesh):
    seq_count = mesh.shape["seq"]

    def body(*args):
        return local(*args, seq_count)

    return jax.shard_map(
        body,
        mesh=mesh,
        in_specs=(
            P("seq", "mp"),
            P("mp"),
            P("seq", None, None, "mp"),
            P("mp"),
            P("seq", "mp"),
            P(),
            P(),
        ),
        out_specs=(P("seq", "mp"), P("seq", None, None, "mp")),
        check_vma=False,
    )
```

```python
import math

import jax
import jax.numpy as jnp
from jax import lax
from jax.experimental import pallas as pl
from jax.experimental.pallas import tpu as pltpu
from jax.sharding import PartitionSpec as P

D = 5120
HEAD_DIM = 128


EPS = 1e-06
MASKED = -1e30


HEADS_PER_STEP = 2


def attend_kernel(tok_slot_ref, q_ref, k_ref, v_ref, g_ref, dq_ref, dk_ref, dv_ref):
    score_scale = 1.0 / math.sqrt(HEAD_DIM)
    depth = k_ref.shape[0] // 2
    in_first = tok_slot_ref[...] == 0
    nt = (((1,), (1,)), ((), ()))
    tn = (((0,), (0,)), ((), ()))
    for head in range(HEADS_PER_STEP):
        cols = slice(head * HEAD_DIM, (head + 1) * HEAD_DIM)
        q = q_ref[:, cols]
        g = g_ref[:, cols]
        k0 = k_ref[:depth, cols]
        k1 = k_ref[depth:, cols]
        v0 = v_ref[:depth, cols]
        v1 = v_ref[depth:, cols]
        scores = jnp.where(
            in_first,
            lax.dot_general(q, k0, nt, preferred_element_type=jnp.float32),
            lax.dot_general(q, k1, nt, preferred_element_type=jnp.float32),
        ) * score_scale
        row_max = jnp.max(scores, axis=1, keepdims=True)
        weights = jnp.exp(scores - row_max)
        normed = weights * (1.0 / jnp.sum(weights, axis=1, keepdims=True))
        weights_low = normed.astype(jnp.bfloat16)
        attended = jnp.where(
            in_first,
            jnp.dot(weights_low, v0, preferred_element_type=jnp.float32),
            jnp.dot(weights_low, v1, preferred_element_type=jnp.float32),
        ).astype(jnp.bfloat16)
        delta = jnp.sum(g.astype(jnp.float32) * attended.astype(jnp.float32), axis=1, keepdims=True)
        grad_weights = jnp.where(
            in_first,
            lax.dot_general(g, v0, nt, preferred_element_type=jnp.float32),
            lax.dot_general(g, v1, nt, preferred_element_type=jnp.float32),
        )
        grad_scores = (normed * (grad_weights - delta) * score_scale).astype(jnp.bfloat16)
        dq_ref[:, cols] = jnp.where(
            in_first,
            jnp.dot(grad_scores, k0, preferred_element_type=jnp.float32),
            jnp.dot(grad_scores, k1, preferred_element_type=jnp.float32),
        ).astype(dq_ref.dtype)
        zero = jnp.zeros_like(grad_scores)
        gs0 = jnp.where(in_first, grad_scores, zero)
        gs1 = jnp.where(in_first, zero, grad_scores)
        w0 = jnp.where(in_first, weights_low, zero)
        w1 = jnp.where(in_first, zero, weights_low)
        dk_ref[:depth, cols] = lax.dot_general(gs0, q, tn, preferred_element_type=jnp.float32)
        dk_ref[depth:, cols] = lax.dot_general(gs1, q, tn, preferred_element_type=jnp.float32)
        dv_ref[:depth, cols] = lax.dot_general(w0, g, tn, preferred_element_type=jnp.float32)
        dv_ref[depth:, cols] = lax.dot_general(w1, g, tn, preferred_element_type=jnp.float32)


def attend(tok_slot, query_normed, keys, values, grad_out):
    tok_rows, feat_width = query_normed.shape
    key_rows = keys.shape[0]
    step_width = HEADS_PER_STEP * HEAD_DIM
    tok_spec = pl.BlockSpec((tok_rows, step_width), lambda h: (0, h))
    key_spec = pl.BlockSpec((key_rows, step_width), lambda h: (0, h))
    return pl.pallas_call(
        attend_kernel,
        grid=(feat_width // step_width,),
        in_specs=[
            pl.BlockSpec((tok_rows, 1), lambda h: (0, 0)),
            tok_spec,
            key_spec,
            key_spec,
            tok_spec,
        ],
        out_specs=[tok_spec, key_spec, key_spec],
        out_shape=[
            jax.ShapeDtypeStruct((tok_rows, feat_width), jnp.bfloat16),
            jax.ShapeDtypeStruct((key_rows, feat_width), jnp.float32),
            jax.ShapeDtypeStruct((key_rows, feat_width), jnp.float32),
        ],
        compiler_params=pltpu.CompilerParams(dimension_semantics=("arbitrary",)),
    )(tok_slot, query_normed, keys, values, grad_out)


def local(query, query_gain, cond, key_gain, grad_out, clip_len, clip_owner, seq_count):
    tok_rows, feat_width = query.shape
    clip_count = clip_len.shape[0]
    cond_depth = cond.shape[2]
    piece = cond_depth // seq_count
    my_index = lax.axis_index("seq")
    first_pos = my_index * tok_rows
    position = first_pos + jnp.arange(tok_rows, dtype=jnp.int32)
    starts = jnp.cumsum(clip_len) - clip_len
    clip_of = jnp.sum((position[:, None] >= starts[None, :]).astype(jnp.int32), axis=1) - 1
    device_pos = jnp.arange(seq_count, dtype=jnp.int32) * tok_rows
    device_first = jnp.sum((device_pos[:, None] >= starts[None, :]).astype(jnp.int32), axis=1) - 1
    query_wide = query.astype(jnp.float32)
    own_key = cond[0, 0].astype(jnp.float32)
    sums = lax.psum(
        (jnp.sum(query_wide * query_wide, axis=1), jnp.sum(own_key * own_key, axis=1)), "mp"
    )
    query_scale = lax.rsqrt(sums[0] / D + EPS)
    query_normed = (query_wide * query_scale[:, None] * query_gain).astype(jnp.bfloat16)
    key_scale = lax.rsqrt(sums[1] / D + EPS)
    own_key_normed = (own_key * key_scale[:, None] * key_gain).astype(jnp.bfloat16)
    own_slab = jnp.stack([own_key_normed, cond[0, 1]])
    spread = own_slab.reshape(2, seq_count, piece, feat_width).transpose(1, 0, 2, 3)
    gathered = lax.all_to_all(spread, "seq", 0, 0, tiled=True)
    clip_rows = jnp.take(gathered, clip_owner, axis=0)
    slot_clip = jnp.stack([device_first, device_first + 1], axis=1)
    wanted = jnp.take(clip_rows, jnp.minimum(slot_clip, clip_count - 1), axis=0)
    arrived = lax.all_to_all(wanted, "seq", 0, 0, tiled=True)
    mine = arrived.transpose(1, 2, 0, 3, 4).reshape(2, 2, cond_depth, feat_width)
    keys = mine[:, 0].reshape(2 * cond_depth, feat_width)
    values = mine[:, 1].reshape(2 * cond_depth, feat_width)
    tok_slot = clip_of - device_first[my_index]
    grad_query, key_grad, value_grad = attend(tok_slot[:, None], query_normed, keys, values, grad_out)
    partial = jnp.stack(
        [key_grad.reshape(2, cond_depth, feat_width), value_grad.reshape(2, cond_depth, feat_width)], axis=1
    ).astype(jnp.bfloat16)
    spread_grads = partial.reshape(2, 2, seq_count, piece, feat_width).transpose(2, 0, 1, 3, 4)
    pieces = lax.all_to_all(spread_grads, "seq", 0, 0, tiled=True)
    source_clip = slot_clip.reshape(2 * seq_count)
    onehot = (source_clip[:, None] == jnp.arange(clip_count, dtype=jnp.int32)[None, :]).astype(jnp.bfloat16)
    summed = jnp.einsum(
        "sc,sx->cx", onehot, pieces.reshape(2 * seq_count, -1), preferred_element_type=jnp.float32
    ).astype(jnp.bfloat16).reshape(clip_count, 2, piece, feat_width)
    owns = clip_owner[None, :] == jnp.arange(seq_count, dtype=jnp.int32)[:, None]
    owned_clip = jnp.sum(jnp.where(owns, jnp.arange(clip_count, dtype=jnp.int32)[None, :], 0), axis=1)
    outgoing = jnp.where(
        jnp.any(owns, axis=1)[:, None, None, None], jnp.take(summed, owned_clip, axis=0), jnp.zeros((), jnp.bfloat16)
    )
    returned = lax.all_to_all(outgoing, "seq", 0, 0, tiled=True)
    owned_grads = returned.transpose(1, 0, 2, 3).reshape(2, cond_depth, feat_width)
    return (grad_query, owned_grads[None])


def solution(mesh):
    seq_count = mesh.shape["seq"]

    def body(*args):
        return local(*args, seq_count)

    return jax.shard_map(
        body,
        mesh=mesh,
        in_specs=(
            P("seq", "mp"),
            P("mp"),
            P("seq", None, None, "mp"),
            P("mp"),
            P("seq", "mp"),
            P(),
            P(),
        ),
        out_specs=(P("seq", "mp"), P("seq", None, None, "mp")),
        check_vma=False,
    )
```

```python
import math

import jax
import jax.numpy as jnp
from jax import lax
from jax.experimental import pallas as pl
from jax.experimental.pallas import tpu as pltpu
from jax.sharding import PartitionSpec as P

D = 5120
HEAD_DIM = 128


EPS = 1e-06
MASKED = -1e30


HEADS_PER_STEP = 2


def attend_kernel(tok_slot_ref, q_ref, k_ref, v_ref, g_ref, dq_ref, dk_ref, dv_ref):
    score_scale = 1.0 / math.sqrt(HEAD_DIM)
    depth = k_ref.shape[0] // 2
    in_first = tok_slot_ref[...] == 0
    nt = (((1,), (1,)), ((), ()))
    tn = (((0,), (0,)), ((), ()))
    for head in range(HEADS_PER_STEP):
        cols = slice(head * HEAD_DIM, (head + 1) * HEAD_DIM)
        q = q_ref[:, cols]
        g = g_ref[:, cols]
        k0 = k_ref[:depth, cols]
        k1 = k_ref[depth:, cols]
        v0 = v_ref[:depth, cols]
        v1 = v_ref[depth:, cols]
        scores = jnp.where(
            in_first,
            lax.dot_general(q, k0, nt, preferred_element_type=jnp.float32),
            lax.dot_general(q, k1, nt, preferred_element_type=jnp.float32),
        ) * score_scale
        row_max = jnp.max(scores, axis=1, keepdims=True)
        weights = jnp.exp(scores - row_max)
        normed = weights * (1.0 / jnp.sum(weights, axis=1, keepdims=True))
        weights_low = normed.astype(jnp.bfloat16)
        attended = jnp.where(
            in_first,
            jnp.dot(weights_low, v0, preferred_element_type=jnp.float32),
            jnp.dot(weights_low, v1, preferred_element_type=jnp.float32),
        ).astype(jnp.bfloat16)
        delta = jnp.sum(g.astype(jnp.float32) * attended.astype(jnp.float32), axis=1, keepdims=True)
        grad_weights = jnp.where(
            in_first,
            lax.dot_general(g, v0, nt, preferred_element_type=jnp.float32),
            lax.dot_general(g, v1, nt, preferred_element_type=jnp.float32),
        )
        grad_scores = (normed * (grad_weights - delta) * score_scale).astype(jnp.bfloat16)
        dq_ref[:, cols] = jnp.where(
            in_first,
            jnp.dot(grad_scores, k0, preferred_element_type=jnp.float32),
            jnp.dot(grad_scores, k1, preferred_element_type=jnp.float32),
        ).astype(dq_ref.dtype)
        zero = jnp.zeros_like(grad_scores)
        gs0 = jnp.where(in_first, grad_scores, zero)
        gs1 = jnp.where(in_first, zero, grad_scores)
        w0 = jnp.where(in_first, weights_low, zero)
        w1 = jnp.where(in_first, zero, weights_low)
        dk_ref[:depth, cols] = lax.dot_general(gs0, q, tn, preferred_element_type=jnp.float32)
        dk_ref[depth:, cols] = lax.dot_general(gs1, q, tn, preferred_element_type=jnp.float32)
        dv_ref[:depth, cols] = lax.dot_general(w0, g, tn, preferred_element_type=jnp.float32)
        dv_ref[depth:, cols] = lax.dot_general(w1, g, tn, preferred_element_type=jnp.float32)


def attend(tok_slot, query_normed, keys, values, grad_out):
    tok_rows, feat_width = query_normed.shape
    key_rows = keys.shape[0]
    step_width = HEADS_PER_STEP * HEAD_DIM
    tok_spec = pl.BlockSpec((tok_rows, step_width), lambda h: (0, h))
    key_spec = pl.BlockSpec((key_rows, step_width), lambda h: (0, h))
    return pl.pallas_call(
        attend_kernel,
        grid=(feat_width // step_width,),
        in_specs=[
            pl.BlockSpec((tok_rows, 1), lambda h: (0, 0)),
            tok_spec,
            key_spec,
            key_spec,
            tok_spec,
        ],
        out_specs=[tok_spec, key_spec, key_spec],
        out_shape=[
            jax.ShapeDtypeStruct((tok_rows, feat_width), jnp.bfloat16),
            jax.ShapeDtypeStruct((key_rows, feat_width), jnp.float32),
            jax.ShapeDtypeStruct((key_rows, feat_width), jnp.float32),
        ],
        compiler_params=pltpu.CompilerParams(dimension_semantics=("arbitrary",)),
    )(tok_slot, query_normed, keys, values, grad_out)


def local(query, query_gain, cond, key_gain, grad_out, clip_len, clip_owner, seq_count):
    tok_rows, feat_width = query.shape
    clip_count = clip_len.shape[0]
    cond_depth = cond.shape[2]
    piece = cond_depth // seq_count
    my_index = lax.axis_index("seq")
    first_pos = my_index * tok_rows
    position = first_pos + jnp.arange(tok_rows, dtype=jnp.int32)
    starts = jnp.cumsum(clip_len) - clip_len
    clip_of = jnp.sum((position[:, None] >= starts[None, :]).astype(jnp.int32), axis=1) - 1
    device_pos = jnp.arange(seq_count, dtype=jnp.int32) * tok_rows
    device_first = jnp.sum((device_pos[:, None] >= starts[None, :]).astype(jnp.int32), axis=1) - 1
    query_wide = query.astype(jnp.float32)
    query_sumsq = lax.psum(jnp.sum(query_wide * query_wide, axis=1), "mp")
    query_scale = lax.rsqrt(query_sumsq / D + EPS)
    query_normed = (query_wide * query_scale[:, None] * query_gain).astype(jnp.bfloat16)
    own_slab = cond[0]
    spread = own_slab.reshape(2, seq_count, piece, feat_width).transpose(1, 0, 2, 3)
    gathered = lax.all_to_all(spread, "seq", 0, 0, tiled=True)
    clip_rows = jnp.take(gathered, clip_owner, axis=0)
    slot_clip = jnp.stack([device_first, device_first + 1], axis=1)
    wanted = jnp.take(clip_rows, jnp.minimum(slot_clip, clip_count - 1), axis=0)
    arrived = lax.all_to_all(wanted, "seq", 0, 0, tiled=True)
    mine = arrived.transpose(1, 2, 0, 3, 4).reshape(2, 2, cond_depth, feat_width)
    key_raw = mine[:, 0].reshape(2 * cond_depth, feat_width).astype(jnp.float32)
    key_sumsq = lax.psum(jnp.sum(key_raw * key_raw, axis=1), "mp")
    key_scale = lax.rsqrt(key_sumsq / D + EPS)
    keys = (key_raw * key_scale[:, None] * key_gain).astype(jnp.bfloat16)
    values = mine[:, 1].reshape(2 * cond_depth, feat_width)
    tok_slot = clip_of - device_first[my_index]
    grad_query, key_grad, value_grad = attend(tok_slot[:, None], query_normed, keys, values, grad_out)
    partial = jnp.stack(
        [key_grad.reshape(2, cond_depth, feat_width), value_grad.reshape(2, cond_depth, feat_width)], axis=1
    ).astype(jnp.bfloat16)
    spread_grads = partial.reshape(2, 2, seq_count, piece, feat_width).transpose(2, 0, 1, 3, 4)
    pieces = lax.all_to_all(spread_grads, "seq", 0, 0, tiled=True)
    source_clip = slot_clip.reshape(2 * seq_count)
    onehot = (source_clip[:, None] == jnp.arange(clip_count, dtype=jnp.int32)[None, :]).astype(jnp.bfloat16)
    summed = jnp.einsum(
        "sc,sx->cx", onehot, pieces.reshape(2 * seq_count, -1), preferred_element_type=jnp.float32
    ).astype(jnp.bfloat16).reshape(clip_count, 2, piece, feat_width)
    owns = clip_owner[None, :] == jnp.arange(seq_count, dtype=jnp.int32)[:, None]
    owned_clip = jnp.sum(jnp.where(owns, jnp.arange(clip_count, dtype=jnp.int32)[None, :], 0), axis=1)
    outgoing = jnp.where(
        jnp.any(owns, axis=1)[:, None, None, None], jnp.take(summed, owned_clip, axis=0), jnp.zeros((), jnp.bfloat16)
    )
    returned = lax.all_to_all(outgoing, "seq", 0, 0, tiled=True)
    owned_grads = returned.transpose(1, 0, 2, 3).reshape(2, cond_depth, feat_width)
    return (grad_query, owned_grads[None])


def solution(mesh):
    seq_count = mesh.shape["seq"]

    def body(*args):
        return local(*args, seq_count)

    return jax.shard_map(
        body,
        mesh=mesh,
        in_specs=(
            P("seq", "mp"),
            P("mp"),
            P("seq", None, None, "mp"),
            P("mp"),
            P("seq", "mp"),
            P(),
            P(),
        ),
        out_specs=(P("seq", "mp"), P("seq", None, None, "mp")),
        check_vma=False,
    )
```

```python
import math

import jax
import jax.numpy as jnp
from jax import lax
from jax.experimental import pallas as pl
from jax.experimental.pallas import tpu as pltpu
from jax.sharding import PartitionSpec as P

D = 5120
HEAD_DIM = 128


EPS = 1e-06
MASKED = -1e30


HEADS_PER_STEP = 2


def attend_kernel(tok_slot_ref, q_ref, k_ref, v_ref, g_ref, dq_ref, dk_ref, dv_ref):
    score_scale = 1.0 / math.sqrt(HEAD_DIM)
    depth = k_ref.shape[0] // 2
    in_first = tok_slot_ref[...] == 0
    nt = (((1,), (1,)), ((), ()))
    tn = (((0,), (0,)), ((), ()))
    for head in range(HEADS_PER_STEP):
        cols = slice(head * HEAD_DIM, (head + 1) * HEAD_DIM)
        q = q_ref[:, cols]
        g = g_ref[:, cols]
        k0 = k_ref[:depth, cols]
        k1 = k_ref[depth:, cols]
        v0 = v_ref[:depth, cols]
        v1 = v_ref[depth:, cols]
        scores = jnp.where(
            in_first,
            lax.dot_general(q, k0, nt, preferred_element_type=jnp.float32),
            lax.dot_general(q, k1, nt, preferred_element_type=jnp.float32),
        ) * score_scale
        row_max = jnp.max(scores, axis=1, keepdims=True)
        weights = jnp.exp(scores - row_max)
        normed = weights * (1.0 / jnp.sum(weights, axis=1, keepdims=True))
        weights_low = normed.astype(jnp.bfloat16)
        attended = jnp.where(
            in_first,
            jnp.dot(weights_low, v0, preferred_element_type=jnp.float32),
            jnp.dot(weights_low, v1, preferred_element_type=jnp.float32),
        ).astype(jnp.bfloat16)
        delta = jnp.sum(g.astype(jnp.float32) * attended.astype(jnp.float32), axis=1, keepdims=True)
        grad_weights = jnp.where(
            in_first,
            lax.dot_general(g, v0, nt, preferred_element_type=jnp.float32),
            lax.dot_general(g, v1, nt, preferred_element_type=jnp.float32),
        )
        grad_scores = (normed * (grad_weights - delta) * score_scale).astype(jnp.bfloat16)
        dq_ref[:, cols] = jnp.where(
            in_first,
            jnp.dot(grad_scores, k0, preferred_element_type=jnp.float32),
            jnp.dot(grad_scores, k1, preferred_element_type=jnp.float32),
        ).astype(dq_ref.dtype)
        zero = jnp.zeros_like(grad_scores)
        gs0 = jnp.where(in_first, grad_scores, zero)
        gs1 = jnp.where(in_first, zero, grad_scores)
        w0 = jnp.where(in_first, weights_low, zero)
        w1 = jnp.where(in_first, zero, weights_low)
        low = dk_ref.dtype
        dk_ref[:depth, cols] = lax.dot_general(gs0, q, tn, preferred_element_type=jnp.float32).astype(low)
        dk_ref[depth:, cols] = lax.dot_general(gs1, q, tn, preferred_element_type=jnp.float32).astype(low)
        dv_ref[:depth, cols] = lax.dot_general(w0, g, tn, preferred_element_type=jnp.float32).astype(low)
        dv_ref[depth:, cols] = lax.dot_general(w1, g, tn, preferred_element_type=jnp.float32).astype(low)


def attend(tok_slot, query_normed, keys, values, grad_out):
    tok_rows, feat_width = query_normed.shape
    key_rows = keys.shape[0]
    step_width = HEADS_PER_STEP * HEAD_DIM
    tok_spec = pl.BlockSpec((tok_rows, step_width), lambda h: (0, h))
    key_spec = pl.BlockSpec((key_rows, step_width), lambda h: (0, h))
    return pl.pallas_call(
        attend_kernel,
        grid=(feat_width // step_width,),
        in_specs=[
            pl.BlockSpec((tok_rows, 1), lambda h: (0, 0)),
            tok_spec,
            key_spec,
            key_spec,
            tok_spec,
        ],
        out_specs=[tok_spec, key_spec, key_spec],
        out_shape=[
            jax.ShapeDtypeStruct((tok_rows, feat_width), jnp.bfloat16),
            jax.ShapeDtypeStruct((key_rows, feat_width), jnp.bfloat16),
            jax.ShapeDtypeStruct((key_rows, feat_width), jnp.bfloat16),
        ],
        compiler_params=pltpu.CompilerParams(dimension_semantics=("arbitrary",)),
    )(tok_slot, query_normed, keys, values, grad_out)


def local(query, query_gain, cond, key_gain, grad_out, clip_len, clip_owner, seq_count):
    tok_rows, feat_width = query.shape
    clip_count = clip_len.shape[0]
    cond_depth = cond.shape[2]
    piece = cond_depth // seq_count
    my_index = lax.axis_index("seq")
    first_pos = my_index * tok_rows
    position = first_pos + jnp.arange(tok_rows, dtype=jnp.int32)
    starts = jnp.cumsum(clip_len) - clip_len
    clip_of = jnp.sum((position[:, None] >= starts[None, :]).astype(jnp.int32), axis=1) - 1
    device_pos = jnp.arange(seq_count, dtype=jnp.int32) * tok_rows
    device_first = jnp.sum((device_pos[:, None] >= starts[None, :]).astype(jnp.int32), axis=1) - 1
    query_wide = query.astype(jnp.float32)
    own_key = cond[0, 0].astype(jnp.float32)
    sums = lax.psum(
        (jnp.sum(query_wide * query_wide, axis=1), jnp.sum(own_key * own_key, axis=1)), "mp"
    )
    query_scale = lax.rsqrt(sums[0] / D + EPS)
    query_normed = (query_wide * query_scale[:, None] * query_gain).astype(jnp.bfloat16)
    key_scale = lax.rsqrt(sums[1] / D + EPS)
    own_key_normed = (own_key * key_scale[:, None] * key_gain).astype(jnp.bfloat16)
    own_slab = jnp.stack([own_key_normed, cond[0, 1]])
    spread = own_slab.reshape(2, seq_count, piece, feat_width).transpose(1, 0, 2, 3)
    gathered = lax.all_to_all(spread, "seq", 0, 0, tiled=True)
    slot_clip = jnp.stack([device_first, device_first + 1], axis=1)
    wanted = jnp.take(gathered, clip_owner[jnp.minimum(slot_clip, clip_count - 1)], axis=0)
    arrived = lax.all_to_all(wanted, "seq", 0, 0, tiled=True)
    mine = arrived.transpose(1, 2, 0, 3, 4).reshape(2, 2, cond_depth, feat_width)
    keys = mine[:, 0].reshape(2 * cond_depth, feat_width)
    values = mine[:, 1].reshape(2 * cond_depth, feat_width)
    tok_slot = clip_of - device_first[my_index]
    grad_query, key_grad, value_grad = attend(tok_slot[:, None], query_normed, keys, values, grad_out)
    partial = jnp.stack(
        [key_grad.reshape(2, cond_depth, feat_width), value_grad.reshape(2, cond_depth, feat_width)], axis=1
    )
    spread_grads = partial.reshape(2, 2, seq_count, piece, feat_width).transpose(2, 0, 1, 3, 4)
    pieces = lax.all_to_all(spread_grads, "seq", 0, 0, tiled=True)
    source_clip = slot_clip.reshape(2 * seq_count)
    onehot = (source_clip[:, None] == jnp.arange(clip_count, dtype=jnp.int32)[None, :]).astype(jnp.bfloat16)
    summed = jnp.einsum(
        "sc,sx->cx", onehot, pieces.reshape(2 * seq_count, -1), preferred_element_type=jnp.float32
    ).astype(jnp.bfloat16).reshape(clip_count, 2, piece, feat_width)
    owns = clip_owner[None, :] == jnp.arange(seq_count, dtype=jnp.int32)[:, None]
    owned_clip = jnp.sum(jnp.where(owns, jnp.arange(clip_count, dtype=jnp.int32)[None, :], 0), axis=1)
    outgoing = jnp.where(
        jnp.any(owns, axis=1)[:, None, None, None], jnp.take(summed, owned_clip, axis=0), jnp.zeros((), jnp.bfloat16)
    )
    returned = lax.all_to_all(outgoing, "seq", 0, 0, tiled=True)
    owned_grads = returned.transpose(1, 0, 2, 3).reshape(2, cond_depth, feat_width)
    return (grad_query, owned_grads[None])


def solution(mesh):
    seq_count = mesh.shape["seq"]

    def body(*args):
        return local(*args, seq_count)

    return jax.shard_map(
        body,
        mesh=mesh,
        in_specs=(
            P("seq", "mp"),
            P("mp"),
            P("seq", None, None, "mp"),
            P("mp"),
            P("seq", "mp"),
            P(),
            P(),
        ),
        out_specs=(P("seq", "mp"), P("seq", None, None, "mp")),
        check_vma=False,
    )
```

```python
import math

import jax
import jax.numpy as jnp
from jax import lax
from jax.experimental import pallas as pl
from jax.experimental.pallas import tpu as pltpu
from jax.sharding import PartitionSpec as P

D = 5120
HEAD_DIM = 128


EPS = 1e-06
MASKED = -1e30


HEADS_PER_STEP = 2


def attend_kernel(tok_slot_ref, q_ref, kv_ref, g_ref, dq_ref, dkv_ref):
    score_scale = 1.0 / math.sqrt(HEAD_DIM)
    holders, _, _, piece, _ = kv_ref.shape
    depth = holders * piece
    in_first = tok_slot_ref[...] == 0
    nt = (((1,), (1,)), ((), ()))
    tn = (((0,), (0,)), ((), ()))
    low = dkv_ref.dtype
    for head in range(HEADS_PER_STEP):
        cols = slice(head * HEAD_DIM, (head + 1) * HEAD_DIM)
        q = q_ref[:, cols]
        g = g_ref[:, cols]
        k0 = kv_ref[:, 0, 0, :, cols].reshape(depth, HEAD_DIM)
        k1 = kv_ref[:, 1, 0, :, cols].reshape(depth, HEAD_DIM)
        v0 = kv_ref[:, 0, 1, :, cols].reshape(depth, HEAD_DIM)
        v1 = kv_ref[:, 1, 1, :, cols].reshape(depth, HEAD_DIM)
        scores = jnp.where(
            in_first,
            lax.dot_general(q, k0, nt, preferred_element_type=jnp.float32),
            lax.dot_general(q, k1, nt, preferred_element_type=jnp.float32),
        ) * score_scale
        row_max = jnp.max(scores, axis=1, keepdims=True)
        weights = jnp.exp(scores - row_max)
        normed = weights * (1.0 / jnp.sum(weights, axis=1, keepdims=True))
        weights_low = normed.astype(jnp.bfloat16)
        attended = jnp.where(
            in_first,
            jnp.dot(weights_low, v0, preferred_element_type=jnp.float32),
            jnp.dot(weights_low, v1, preferred_element_type=jnp.float32),
        ).astype(jnp.bfloat16)
        delta = jnp.sum(g.astype(jnp.float32) * attended.astype(jnp.float32), axis=1, keepdims=True)
        grad_weights = jnp.where(
            in_first,
            lax.dot_general(g, v0, nt, preferred_element_type=jnp.float32),
            lax.dot_general(g, v1, nt, preferred_element_type=jnp.float32),
        )
        grad_scores = (normed * (grad_weights - delta) * score_scale).astype(jnp.bfloat16)
        dq_ref[:, cols] = jnp.where(
            in_first,
            jnp.dot(grad_scores, k0, preferred_element_type=jnp.float32),
            jnp.dot(grad_scores, k1, preferred_element_type=jnp.float32),
        ).astype(dq_ref.dtype)
        zero = jnp.zeros_like(grad_scores)
        gs0 = jnp.where(in_first, grad_scores, zero)
        gs1 = jnp.where(in_first, zero, grad_scores)
        w0 = jnp.where(in_first, weights_low, zero)
        w1 = jnp.where(in_first, zero, weights_low)
        for slot, (gs, w) in enumerate(((gs0, w0), (gs1, w1))):
            dk = lax.dot_general(gs, q, tn, preferred_element_type=jnp.float32).astype(low)
            dv = lax.dot_general(w, g, tn, preferred_element_type=jnp.float32).astype(low)
            dkv_ref[:, slot, 0, :, cols] = dk.reshape(holders, piece, HEAD_DIM)
            dkv_ref[:, slot, 1, :, cols] = dv.reshape(holders, piece, HEAD_DIM)


def attend(tok_slot, query_normed, kv, grad_out):
    tok_rows, feat_width = query_normed.shape
    step_width = HEADS_PER_STEP * HEAD_DIM
    tok_spec = pl.BlockSpec((tok_rows, step_width), lambda h: (0, h))
    kv_spec = pl.BlockSpec(kv.shape[:4] + (step_width,), lambda h: (0, 0, 0, 0, h))
    return pl.pallas_call(
        attend_kernel,
        grid=(feat_width // step_width,),
        in_specs=[
            pl.BlockSpec((tok_rows, 1), lambda h: (0, 0)),
            tok_spec,
            kv_spec,
            tok_spec,
        ],
        out_specs=[tok_spec, kv_spec],
        out_shape=[
            jax.ShapeDtypeStruct((tok_rows, feat_width), jnp.bfloat16),
            jax.ShapeDtypeStruct(kv.shape, jnp.bfloat16),
        ],
        compiler_params=pltpu.CompilerParams(dimension_semantics=("arbitrary",)),
    )(tok_slot, query_normed, kv, grad_out)


def local(query, query_gain, cond, key_gain, grad_out, clip_len, clip_owner, seq_count):
    tok_rows, feat_width = query.shape
    clip_count = clip_len.shape[0]
    cond_depth = cond.shape[2]
    piece = cond_depth // seq_count
    my_index = lax.axis_index("seq")
    first_pos = my_index * tok_rows
    position = first_pos + jnp.arange(tok_rows, dtype=jnp.int32)
    starts = jnp.cumsum(clip_len) - clip_len
    clip_of = jnp.sum((position[:, None] >= starts[None, :]).astype(jnp.int32), axis=1) - 1
    device_pos = jnp.arange(seq_count, dtype=jnp.int32) * tok_rows
    device_first = jnp.sum((device_pos[:, None] >= starts[None, :]).astype(jnp.int32), axis=1) - 1
    query_wide = query.astype(jnp.float32)
    own_key = cond[0, 0].astype(jnp.float32)
    sums = lax.psum(
        (jnp.sum(query_wide * query_wide, axis=1), jnp.sum(own_key * own_key, axis=1)), "mp"
    )
    query_scale = lax.rsqrt(sums[0] / D + EPS)
    query_normed = (query_wide * query_scale[:, None] * query_gain).astype(jnp.bfloat16)
    key_scale = lax.rsqrt(sums[1] / D + EPS)
    own_key_normed = (own_key * key_scale[:, None] * key_gain).astype(jnp.bfloat16)
    own_slab = jnp.stack([own_key_normed, cond[0, 1]])
    spread = own_slab.reshape(2, seq_count, piece, feat_width).transpose(1, 0, 2, 3)
    gathered = lax.all_to_all(spread, "seq", 0, 0, tiled=True)
    slot_clip = jnp.stack([device_first, device_first + 1], axis=1)
    wanted = jnp.take(gathered, clip_owner[jnp.minimum(slot_clip, clip_count - 1)], axis=0)
    arrived = lax.all_to_all(wanted, "seq", 0, 0, tiled=True)
    tok_slot = clip_of - device_first[my_index]
    if piece % 16 == 0:
        grad_query, spread_grads = attend(tok_slot[:, None], query_normed, arrived, grad_out)
    else:
        mine = arrived.transpose(1, 2, 0, 3, 4).reshape(1, 2, 2, cond_depth, feat_width)
        grad_query, grad_slots = attend(tok_slot[:, None], query_normed, mine, grad_out)
        spread_grads = grad_slots[0].reshape(2, 2, seq_count, piece, feat_width).transpose(2, 0, 1, 3, 4)
    pieces = lax.all_to_all(spread_grads, "seq", 0, 0, tiled=True)
    source_clip = slot_clip.reshape(2 * seq_count)
    onehot = (source_clip[:, None] == jnp.arange(clip_count, dtype=jnp.int32)[None, :]).astype(jnp.bfloat16)
    summed = jnp.einsum(
        "sc,sx->cx", onehot, pieces.reshape(2 * seq_count, -1), preferred_element_type=jnp.float32
    ).astype(jnp.bfloat16).reshape(clip_count, 2, piece, feat_width)
    owns = clip_owner[None, :] == jnp.arange(seq_count, dtype=jnp.int32)[:, None]
    owned_clip = jnp.sum(jnp.where(owns, jnp.arange(clip_count, dtype=jnp.int32)[None, :], 0), axis=1)
    outgoing = jnp.where(
        jnp.any(owns, axis=1)[:, None, None, None], jnp.take(summed, owned_clip, axis=0), jnp.zeros((), jnp.bfloat16)
    )
    returned = lax.all_to_all(outgoing, "seq", 0, 0, tiled=True)
    owned_grads = returned.transpose(1, 0, 2, 3).reshape(2, cond_depth, feat_width)
    return (grad_query, owned_grads[None])


def solution(mesh):
    seq_count = mesh.shape["seq"]

    def body(*args):
        return local(*args, seq_count)

    return jax.shard_map(
        body,
        mesh=mesh,
        in_specs=(
            P("seq", "mp"),
            P("mp"),
            P("seq", None, None, "mp"),
            P("mp"),
            P("seq", "mp"),
            P(),
            P(),
        ),
        out_specs=(P("seq", "mp"), P("seq", None, None, "mp")),
        check_vma=False,
    )
```

```python
import math

import jax
import jax.numpy as jnp
from jax import lax
from jax.experimental import pallas as pl
from jax.experimental.pallas import tpu as pltpu
from jax.sharding import PartitionSpec as P

D = 5120
HEAD_DIM = 128


EPS = 1e-06
MASKED = -1e30


HEADS_PER_STEP = 2


def attend_kernel(tok_slot_ref, q_ref, kv_ref, g_ref, dq_ref, dkv_ref):
    score_scale = 1.0 / math.sqrt(HEAD_DIM)
    holders, _, _, piece, _ = kv_ref.shape
    depth = holders * piece
    in_first = tok_slot_ref[...] == 0
    nt = (((1,), (1,)), ((), ()))
    tn = (((0,), (0,)), ((), ()))
    low = dkv_ref.dtype
    for head in range(HEADS_PER_STEP):
        cols = slice(head * HEAD_DIM, (head + 1) * HEAD_DIM)
        q = q_ref[:, cols]
        g = g_ref[:, cols]
        k0 = kv_ref[:, 0, 0, :, cols].reshape(depth, HEAD_DIM)
        k1 = kv_ref[:, 1, 0, :, cols].reshape(depth, HEAD_DIM)
        v0 = kv_ref[:, 0, 1, :, cols].reshape(depth, HEAD_DIM)
        v1 = kv_ref[:, 1, 1, :, cols].reshape(depth, HEAD_DIM)
        scores = jnp.where(
            in_first,
            lax.dot_general(q, k0, nt, preferred_element_type=jnp.float32),
            lax.dot_general(q, k1, nt, preferred_element_type=jnp.float32),
        ) * score_scale
        row_max = jnp.max(scores, axis=1, keepdims=True)
        weights = jnp.exp(scores - row_max)
        normed = weights * (1.0 / jnp.sum(weights, axis=1, keepdims=True))
        weights_low = normed.astype(jnp.bfloat16)
        attended = jnp.where(
            in_first,
            jnp.dot(weights_low, v0, preferred_element_type=jnp.float32),
            jnp.dot(weights_low, v1, preferred_element_type=jnp.float32),
        ).astype(jnp.bfloat16)
        delta = jnp.sum(g.astype(jnp.float32) * attended.astype(jnp.float32), axis=1, keepdims=True)
        grad_weights = jnp.where(
            in_first,
            lax.dot_general(g, v0, nt, preferred_element_type=jnp.float32),
            lax.dot_general(g, v1, nt, preferred_element_type=jnp.float32),
        )
        grad_scores = (normed * (grad_weights - delta) * score_scale).astype(jnp.bfloat16)
        dq_ref[:, cols] = jnp.where(
            in_first,
            jnp.dot(grad_scores, k0, preferred_element_type=jnp.float32),
            jnp.dot(grad_scores, k1, preferred_element_type=jnp.float32),
        ).astype(dq_ref.dtype)
        zero = jnp.zeros_like(grad_scores)
        gs0 = jnp.where(in_first, grad_scores, zero)
        gs1 = jnp.where(in_first, zero, grad_scores)
        w0 = jnp.where(in_first, weights_low, zero)
        w1 = jnp.where(in_first, zero, weights_low)
        for slot, (gs, w) in enumerate(((gs0, w0), (gs1, w1))):
            dk = lax.dot_general(gs, q, tn, preferred_element_type=jnp.float32).astype(low)
            dv = lax.dot_general(w, g, tn, preferred_element_type=jnp.float32).astype(low)
            dkv_ref[:, slot, 0, :, cols] = dk.reshape(holders, piece, HEAD_DIM)
            dkv_ref[:, slot, 1, :, cols] = dv.reshape(holders, piece, HEAD_DIM)


def attend(tok_slot, query_normed, kv, grad_out):
    tok_rows, feat_width = query_normed.shape
    step_width = HEADS_PER_STEP * HEAD_DIM
    tok_spec = pl.BlockSpec((tok_rows, step_width), lambda h: (0, h))
    kv_spec = pl.BlockSpec(kv.shape[:4] + (step_width,), lambda h: (0, 0, 0, 0, h))
    return pl.pallas_call(
        attend_kernel,
        grid=(feat_width // step_width,),
        in_specs=[
            pl.BlockSpec((tok_rows, 1), lambda h: (0, 0)),
            tok_spec,
            kv_spec,
            tok_spec,
        ],
        out_specs=[tok_spec, kv_spec],
        out_shape=[
            jax.ShapeDtypeStruct((tok_rows, feat_width), jnp.bfloat16),
            jax.ShapeDtypeStruct(kv.shape, jnp.bfloat16),
        ],
        compiler_params=pltpu.CompilerParams(dimension_semantics=("arbitrary",)),
    )(tok_slot, query_normed, kv, grad_out)


def local(query, query_gain, cond, key_gain, grad_out, clip_len, clip_owner, seq_count):
    tok_rows, feat_width = query.shape
    clip_count = clip_len.shape[0]
    cond_depth = cond.shape[2]
    piece = cond_depth // seq_count
    my_index = lax.axis_index("seq")
    first_pos = my_index * tok_rows
    position = first_pos + jnp.arange(tok_rows, dtype=jnp.int32)
    starts = jnp.cumsum(clip_len) - clip_len
    clip_of = jnp.sum((position[:, None] >= starts[None, :]).astype(jnp.int32), axis=1) - 1
    device_pos = jnp.arange(seq_count, dtype=jnp.int32) * tok_rows
    device_first = jnp.sum((device_pos[:, None] >= starts[None, :]).astype(jnp.int32), axis=1) - 1
    query_wide = query.astype(jnp.float32)
    own_key = cond[0, 0].astype(jnp.float32)
    sums = lax.psum(
        (jnp.sum(query_wide * query_wide, axis=1), jnp.sum(own_key * own_key, axis=1)), "mp"
    )
    query_scale = lax.rsqrt(sums[0] / D + EPS)
    query_normed = (query_wide * query_scale[:, None] * query_gain).astype(jnp.bfloat16)
    key_scale = lax.rsqrt(sums[1] / D + EPS)
    own_key_normed = (own_key * key_scale[:, None] * key_gain).astype(jnp.bfloat16)
    own_slab = jnp.stack([own_key_normed, cond[0, 1]])
    spread = own_slab.reshape(2, seq_count, piece, feat_width)
    gathered = lax.all_to_all(spread, "seq", 1, 0, tiled=True).reshape(seq_count, 2, piece, feat_width)
    slot_clip = jnp.stack([device_first, device_first + 1], axis=1)
    wanted = jnp.take(gathered, clip_owner[jnp.minimum(slot_clip, clip_count - 1)], axis=0, mode="clip")
    arrived = lax.all_to_all(wanted, "seq", 0, 0, tiled=True)
    tok_slot = clip_of - device_first[my_index]
    if piece % 16 == 0:
        grad_query, spread_grads = attend(tok_slot[:, None], query_normed, arrived, grad_out)
    else:
        mine = arrived.transpose(1, 2, 0, 3, 4).reshape(1, 2, 2, cond_depth, feat_width)
        grad_query, grad_slots = attend(tok_slot[:, None], query_normed, mine, grad_out)
        spread_grads = grad_slots[0].reshape(2, 2, seq_count, piece, feat_width).transpose(2, 0, 1, 3, 4)
    pieces = lax.all_to_all(spread_grads, "seq", 0, 0, tiled=True)
    source_clip = slot_clip.reshape(2 * seq_count)
    onehot = (source_clip[:, None] == jnp.arange(clip_count, dtype=jnp.int32)[None, :]).astype(jnp.bfloat16)
    summed = jnp.einsum(
        "sc,sx->cx", onehot, pieces.reshape(2 * seq_count, -1), preferred_element_type=jnp.float32
    ).astype(jnp.bfloat16).reshape(clip_count, 2, piece, feat_width)
    owns = clip_owner[None, :] == jnp.arange(seq_count, dtype=jnp.int32)[:, None]
    owned_clip = jnp.sum(jnp.where(owns, jnp.arange(clip_count, dtype=jnp.int32)[None, :], 0), axis=1)
    outgoing = jnp.where(
        jnp.any(owns, axis=1)[:, None, None, None], jnp.take(summed, owned_clip, axis=0, mode="clip"), jnp.zeros((), jnp.bfloat16)
    )
    owned_grads = lax.all_to_all(outgoing, "seq", 0, 2, tiled=True).reshape(2, cond_depth, feat_width)
    return (grad_query, owned_grads[None])


def solution(mesh):
    seq_count = mesh.shape["seq"]

    def body(*args):
        return local(*args, seq_count)

    return jax.shard_map(
        body,
        mesh=mesh,
        in_specs=(
            P("seq", "mp"),
            P("mp"),
            P("seq", None, None, "mp"),
            P("mp"),
            P("seq", "mp"),
            P(),
            P(),
        ),
        out_specs=(P("seq", "mp"), P("seq", None, None, "mp")),
        check_vma=False,
    )
```

```python
import math

import jax
import jax.numpy as jnp
from jax import lax
from jax.experimental import pallas as pl
from jax.experimental.pallas import tpu as pltpu
from jax.sharding import PartitionSpec as P

D = 5120
HEAD_DIM = 128


EPS = 1e-06
MASKED = -1e30


HEADS_PER_STEP = 2


def attend_kernel(tok_slot_ref, q_ref, kv_ref, g_ref, gs_ref, dkv_ref):
    score_scale = 1.0 / math.sqrt(HEAD_DIM)
    holders, _, _, piece, _ = kv_ref.shape
    depth = holders * piece
    in_first = tok_slot_ref[...] == 0
    nt = (((1,), (1,)), ((), ()))
    tn = (((0,), (0,)), ((), ()))
    low = dkv_ref.dtype
    for head in range(HEADS_PER_STEP):
        cols = slice(head * HEAD_DIM, (head + 1) * HEAD_DIM)
        q = q_ref[:, cols]
        g = g_ref[:, cols]
        k0 = kv_ref[:, 0, 0, :, cols].reshape(depth, HEAD_DIM)
        k1 = kv_ref[:, 1, 0, :, cols].reshape(depth, HEAD_DIM)
        v0 = kv_ref[:, 0, 1, :, cols].reshape(depth, HEAD_DIM)
        v1 = kv_ref[:, 1, 1, :, cols].reshape(depth, HEAD_DIM)
        scores = jnp.where(
            in_first,
            lax.dot_general(q, k0, nt, preferred_element_type=jnp.float32),
            lax.dot_general(q, k1, nt, preferred_element_type=jnp.float32),
        ) * score_scale
        row_max = jnp.max(scores, axis=1, keepdims=True)
        weights = jnp.exp(scores - row_max)
        normed = weights * (1.0 / jnp.sum(weights, axis=1, keepdims=True))
        weights_low = normed.astype(jnp.bfloat16)
        attended = jnp.where(
            in_first,
            jnp.dot(weights_low, v0, preferred_element_type=jnp.float32),
            jnp.dot(weights_low, v1, preferred_element_type=jnp.float32),
        ).astype(jnp.bfloat16)
        delta = jnp.sum(g.astype(jnp.float32) * attended.astype(jnp.float32), axis=1, keepdims=True)
        grad_weights = jnp.where(
            in_first,
            lax.dot_general(g, v0, nt, preferred_element_type=jnp.float32),
            lax.dot_general(g, v1, nt, preferred_element_type=jnp.float32),
        )
        grad_scores = (normed * (grad_weights - delta) * score_scale).astype(jnp.bfloat16)
        gs_ref[:, cols] = grad_scores
        zero = jnp.zeros_like(grad_scores)
        gs0 = jnp.where(in_first, grad_scores, zero)
        gs1 = jnp.where(in_first, zero, grad_scores)
        w0 = jnp.where(in_first, weights_low, zero)
        w1 = jnp.where(in_first, zero, weights_low)
        for slot, (gs, w) in enumerate(((gs0, w0), (gs1, w1))):
            dk = lax.dot_general(gs, q, tn, preferred_element_type=jnp.float32).astype(low)
            dv = lax.dot_general(w, g, tn, preferred_element_type=jnp.float32).astype(low)
            dkv_ref[:, slot, 0, :, cols] = dk.reshape(holders, piece, HEAD_DIM)
            dkv_ref[:, slot, 1, :, cols] = dv.reshape(holders, piece, HEAD_DIM)


def grad_query_kernel(tok_slot_ref, gs_ref, kv_ref, dq_ref):
    holders, _, _, piece, _ = kv_ref.shape
    depth = holders * piece
    in_first = tok_slot_ref[...] == 0
    for head in range(HEADS_PER_STEP):
        cols = slice(head * HEAD_DIM, (head + 1) * HEAD_DIM)
        grad_scores = gs_ref[:, cols]
        k0 = kv_ref[:, 0, 0, :, cols].reshape(depth, HEAD_DIM)
        k1 = kv_ref[:, 1, 0, :, cols].reshape(depth, HEAD_DIM)
        dq_ref[:, cols] = jnp.where(
            in_first,
            jnp.dot(grad_scores, k0, preferred_element_type=jnp.float32),
            jnp.dot(grad_scores, k1, preferred_element_type=jnp.float32),
        ).astype(dq_ref.dtype)


def attend(tok_slot, query_normed, kv, grad_out):
    tok_rows, feat_width = query_normed.shape
    step_width = HEADS_PER_STEP * HEAD_DIM
    tok_spec = pl.BlockSpec((tok_rows, step_width), lambda h: (0, h))
    kv_spec = pl.BlockSpec(kv.shape[:4] + (step_width,), lambda h: (0, 0, 0, 0, h))
    grad_scores, grad_kv = pl.pallas_call(
        attend_kernel,
        grid=(feat_width // step_width,),
        in_specs=[
            pl.BlockSpec((tok_rows, 1), lambda h: (0, 0)),
            tok_spec,
            kv_spec,
            tok_spec,
        ],
        out_specs=[tok_spec, kv_spec],
        out_shape=[
            jax.ShapeDtypeStruct((tok_rows, feat_width), jnp.bfloat16),
            jax.ShapeDtypeStruct(kv.shape, jnp.bfloat16),
        ],
        compiler_params=pltpu.CompilerParams(dimension_semantics=("arbitrary",)),
    )(tok_slot, query_normed, kv, grad_out)
    grad_query = pl.pallas_call(
        grad_query_kernel,
        grid=(feat_width // step_width,),
        in_specs=[pl.BlockSpec((tok_rows, 1), lambda h: (0, 0)), tok_spec, kv_spec],
        out_specs=tok_spec,
        out_shape=jax.ShapeDtypeStruct((tok_rows, feat_width), jnp.bfloat16),
        compiler_params=pltpu.CompilerParams(dimension_semantics=("arbitrary",)),
    )(tok_slot, grad_scores, kv)
    return grad_query, grad_kv


def local(query, query_gain, cond, key_gain, grad_out, clip_len, clip_owner, seq_count):
    tok_rows, feat_width = query.shape
    clip_count = clip_len.shape[0]
    cond_depth = cond.shape[2]
    piece = cond_depth // seq_count
    my_index = lax.axis_index("seq")
    first_pos = my_index * tok_rows
    position = first_pos + jnp.arange(tok_rows, dtype=jnp.int32)
    starts = jnp.cumsum(clip_len) - clip_len
    clip_of = jnp.sum((position[:, None] >= starts[None, :]).astype(jnp.int32), axis=1) - 1
    device_pos = jnp.arange(seq_count, dtype=jnp.int32) * tok_rows
    device_first = jnp.sum((device_pos[:, None] >= starts[None, :]).astype(jnp.int32), axis=1) - 1
    query_wide = query.astype(jnp.float32)
    own_key = cond[0, 0].astype(jnp.float32)
    sums = lax.psum(
        (jnp.sum(query_wide * query_wide, axis=1), jnp.sum(own_key * own_key, axis=1)), "mp"
    )
    query_scale = lax.rsqrt(sums[0] / D + EPS)
    query_normed = (query_wide * query_scale[:, None] * query_gain).astype(jnp.bfloat16)
    key_scale = lax.rsqrt(sums[1] / D + EPS)
    own_key_normed = (own_key * key_scale[:, None] * key_gain).astype(jnp.bfloat16)
    own_slab = jnp.stack([own_key_normed, cond[0, 1]])
    spread = own_slab.reshape(2, seq_count, piece, feat_width)
    gathered = lax.all_to_all(spread, "seq", 1, 0, tiled=True).reshape(seq_count, 2, piece, feat_width)
    slot_clip = jnp.stack([device_first, device_first + 1], axis=1)
    wanted = jnp.take(gathered, clip_owner[jnp.minimum(slot_clip, clip_count - 1)], axis=0, mode="clip")
    arrived = lax.all_to_all(wanted, "seq", 0, 0, tiled=True)
    tok_slot = clip_of - device_first[my_index]
    if piece % 16 == 0:
        grad_query, spread_grads = attend(tok_slot[:, None], query_normed, arrived, grad_out)
    else:
        mine = arrived.transpose(1, 2, 0, 3, 4).reshape(1, 2, 2, cond_depth, feat_width)
        grad_query, grad_slots = attend(tok_slot[:, None], query_normed, mine, grad_out)
        spread_grads = grad_slots[0].reshape(2, 2, seq_count, piece, feat_width).transpose(2, 0, 1, 3, 4)
    pieces = lax.all_to_all(spread_grads, "seq", 0, 0, tiled=True)
    source_clip = slot_clip.reshape(2 * seq_count)
    onehot = (source_clip[:, None] == jnp.arange(clip_count, dtype=jnp.int32)[None, :]).astype(jnp.bfloat16)
    summed = jnp.einsum(
        "sc,sx->cx", onehot, pieces.reshape(2 * seq_count, -1), preferred_element_type=jnp.float32
    ).astype(jnp.bfloat16).reshape(clip_count, 2, piece, feat_width)
    owns = clip_owner[None, :] == jnp.arange(seq_count, dtype=jnp.int32)[:, None]
    owned_clip = jnp.sum(jnp.where(owns, jnp.arange(clip_count, dtype=jnp.int32)[None, :], 0), axis=1)
    outgoing = jnp.where(
        jnp.any(owns, axis=1)[:, None, None, None], jnp.take(summed, owned_clip, axis=0, mode="clip"), jnp.zeros((), jnp.bfloat16)
    )
    owned_grads = lax.all_to_all(outgoing, "seq", 0, 2, tiled=True).reshape(2, cond_depth, feat_width)
    return (grad_query, owned_grads[None])


def solution(mesh):
    seq_count = mesh.shape["seq"]

    def body(*args):
        return local(*args, seq_count)

    return jax.shard_map(
        body,
        mesh=mesh,
        in_specs=(
            P("seq", "mp"),
            P("mp"),
            P("seq", None, None, "mp"),
            P("mp"),
            P("seq", "mp"),
            P(),
            P(),
        ),
        out_specs=(P("seq", "mp"), P("seq", None, None, "mp")),
        check_vma=False,
    )
```

```python
import math

import jax
import jax.numpy as jnp
from jax import lax
from jax.experimental import pallas as pl
from jax.experimental.pallas import tpu as pltpu
from jax.sharding import PartitionSpec as P

D = 5120
HEAD_DIM = 128


EPS = 1e-06
MASKED = -1e30


HEADS_PER_STEP = 2


def attend_kernel(tok_slot_ref, q_ref, kv_ref, g_ref, dq_ref, dkv_ref):
    score_scale = 1.0 / math.sqrt(HEAD_DIM)
    holders, _, _, piece, _ = kv_ref.shape
    depth = holders * piece
    in_first = tok_slot_ref[...] == 0
    nt = (((1,), (1,)), ((), ()))
    tn = (((0,), (0,)), ((), ()))
    low = dkv_ref.dtype
    for head in range(HEADS_PER_STEP):
        cols = slice(head * HEAD_DIM, (head + 1) * HEAD_DIM)
        q = q_ref[:, cols]
        g = g_ref[:, cols]
        k0 = kv_ref[:, 0, 0, :, cols].reshape(depth, HEAD_DIM)
        k1 = kv_ref[:, 1, 0, :, cols].reshape(depth, HEAD_DIM)
        v0 = kv_ref[:, 0, 1, :, cols].reshape(depth, HEAD_DIM)
        v1 = kv_ref[:, 1, 1, :, cols].reshape(depth, HEAD_DIM)
        scores = jnp.where(
            in_first,
            lax.dot_general(q, k0, nt, preferred_element_type=jnp.float32),
            lax.dot_general(q, k1, nt, preferred_element_type=jnp.float32),
        ) * score_scale
        row_max = jnp.max(scores, axis=1, keepdims=True)
        weights = jnp.exp(scores - row_max)
        normed = weights * (1.0 / jnp.sum(weights, axis=1, keepdims=True))
        weights_low = normed.astype(jnp.bfloat16)
        attended = jnp.where(
            in_first,
            jnp.dot(weights_low, v0, preferred_element_type=jnp.float32),
            jnp.dot(weights_low, v1, preferred_element_type=jnp.float32),
        ).astype(jnp.bfloat16)
        delta = jnp.sum(g.astype(jnp.float32) * attended.astype(jnp.float32), axis=1, keepdims=True)
        grad_weights = jnp.where(
            in_first,
            lax.dot_general(g, v0, nt, preferred_element_type=jnp.float32),
            lax.dot_general(g, v1, nt, preferred_element_type=jnp.float32),
        )
        grad_scores = (normed * (grad_weights - delta) * score_scale).astype(jnp.bfloat16)
        dq_ref[:, cols] = jnp.where(
            in_first,
            jnp.dot(grad_scores, k0, preferred_element_type=jnp.float32),
            jnp.dot(grad_scores, k1, preferred_element_type=jnp.float32),
        ).astype(dq_ref.dtype)
        zero = jnp.zeros_like(grad_scores)
        gs0 = jnp.where(in_first, grad_scores, zero)
        gs1 = jnp.where(in_first, zero, grad_scores)
        w0 = jnp.where(in_first, weights_low, zero)
        w1 = jnp.where(in_first, zero, weights_low)
        for slot, (gs, w) in enumerate(((gs0, w0), (gs1, w1))):
            dk = lax.dot_general(gs, q, tn, preferred_element_type=jnp.float32).astype(low)
            dv = lax.dot_general(w, g, tn, preferred_element_type=jnp.float32).astype(low)
            dkv_ref[:, slot, 0, :, cols] = dk.reshape(holders, piece, HEAD_DIM)
            dkv_ref[:, slot, 1, :, cols] = dv.reshape(holders, piece, HEAD_DIM)


def attend(tok_slot, query_normed, kv, grad_out):
    tok_rows, feat_width = query_normed.shape
    step_width = HEADS_PER_STEP * HEAD_DIM
    tok_spec = pl.BlockSpec((tok_rows, step_width), lambda h: (0, h))
    kv_spec = pl.BlockSpec(kv.shape[:4] + (step_width,), lambda h: (0, 0, 0, 0, h))
    return pl.pallas_call(
        attend_kernel,
        grid=(feat_width // step_width,),
        in_specs=[
            pl.BlockSpec((tok_rows, 1), lambda h: (0, 0)),
            tok_spec,
            kv_spec,
            tok_spec,
        ],
        out_specs=[tok_spec, kv_spec],
        out_shape=[
            jax.ShapeDtypeStruct((tok_rows, feat_width), jnp.bfloat16),
            jax.ShapeDtypeStruct(kv.shape, jnp.bfloat16),
        ],
        compiler_params=pltpu.CompilerParams(dimension_semantics=("arbitrary",)),
    )(tok_slot, query_normed, kv, grad_out)


def local(query, query_gain, cond, key_gain, grad_out, clip_len, clip_owner, seq_count):
    tok_rows, feat_width = query.shape
    clip_count = clip_len.shape[0]
    cond_depth = cond.shape[2]
    piece = cond_depth // seq_count
    my_index = lax.axis_index("seq")
    first_pos = my_index * tok_rows
    position = first_pos + jnp.arange(tok_rows, dtype=jnp.int32)
    starts = jnp.cumsum(clip_len) - clip_len
    clip_of = jnp.sum((position[:, None] >= starts[None, :]).astype(jnp.int32), axis=1) - 1
    device_pos = jnp.arange(seq_count, dtype=jnp.int32) * tok_rows
    device_first = jnp.sum((device_pos[:, None] >= starts[None, :]).astype(jnp.int32), axis=1) - 1
    own_key = cond[0, 0].astype(jnp.float32)
    key_scale = lax.rsqrt(lax.psum(jnp.sum(own_key * own_key, axis=1), "mp") / D + EPS)
    own_key_normed = (own_key * key_scale[:, None] * key_gain).astype(jnp.bfloat16)
    own_slab = jnp.stack([own_key_normed, cond[0, 1]])
    spread = own_slab.reshape(2, seq_count, piece, feat_width)
    gathered = lax.all_to_all(spread, "seq", 1, 0, tiled=True).reshape(seq_count, 2, piece, feat_width)
    slot_clip = jnp.stack([device_first, device_first + 1], axis=1)
    wanted = jnp.take(gathered, clip_owner[jnp.minimum(slot_clip, clip_count - 1)], axis=0, mode="clip")
    arrived = lax.all_to_all(wanted, "seq", 0, 0, tiled=True)
    query_wide = query.astype(jnp.float32)
    after_first = (gathered[0, 0, 0, 0] * 0).astype(jnp.float32)
    query_sumsq = lax.psum(jnp.sum(query_wide * query_wide, axis=1) + after_first, "mp")
    query_scale = lax.rsqrt(query_sumsq / D + EPS)
    query_normed = (query_wide * query_scale[:, None] * query_gain).astype(jnp.bfloat16)
    tok_slot = clip_of - device_first[my_index]
    if piece % 16 == 0:
        grad_query, spread_grads = attend(tok_slot[:, None], query_normed, arrived, grad_out)
    else:
        mine = arrived.transpose(1, 2, 0, 3, 4).reshape(1, 2, 2, cond_depth, feat_width)
        grad_query, grad_slots = attend(tok_slot[:, None], query_normed, mine, grad_out)
        spread_grads = grad_slots[0].reshape(2, 2, seq_count, piece, feat_width).transpose(2, 0, 1, 3, 4)
    pieces = lax.all_to_all(spread_grads, "seq", 0, 0, tiled=True)
    source_clip = slot_clip.reshape(2 * seq_count)
    onehot = (source_clip[:, None] == jnp.arange(clip_count, dtype=jnp.int32)[None, :]).astype(jnp.bfloat16)
    summed = jnp.einsum(
        "sc,sx->cx", onehot, pieces.reshape(2 * seq_count, -1), preferred_element_type=jnp.float32
    ).astype(jnp.bfloat16).reshape(clip_count, 2, piece, feat_width)
    owns = clip_owner[None, :] == jnp.arange(seq_count, dtype=jnp.int32)[:, None]
    owned_clip = jnp.sum(jnp.where(owns, jnp.arange(clip_count, dtype=jnp.int32)[None, :], 0), axis=1)
    outgoing = jnp.where(
        jnp.any(owns, axis=1)[:, None, None, None], jnp.take(summed, owned_clip, axis=0, mode="clip"), jnp.zeros((), jnp.bfloat16)
    )
    owned_grads = lax.all_to_all(outgoing, "seq", 0, 2, tiled=True).reshape(2, cond_depth, feat_width)
    return (grad_query, owned_grads[None])


def solution(mesh):
    seq_count = mesh.shape["seq"]

    def body(*args):
        return local(*args, seq_count)

    return jax.shard_map(
        body,
        mesh=mesh,
        in_specs=(
            P("seq", "mp"),
            P("mp"),
            P("seq", None, None, "mp"),
            P("mp"),
            P("seq", "mp"),
            P(),
            P(),
        ),
        out_specs=(P("seq", "mp"), P("seq", None, None, "mp")),
        check_vma=False,
    )
```

```python
import math

import jax
import jax.numpy as jnp
from jax import lax
from jax.experimental import pallas as pl
from jax.experimental.pallas import tpu as pltpu
from jax.sharding import PartitionSpec as P

D = 5120
HEAD_DIM = 128


EPS = 1e-06
MASKED = -1e30


HEADS_PER_STEP = 2


def attend_kernel(tok_slot_ref, q_ref, kv_ref, g_ref, dq_ref, dkv_ref):
    score_scale = 1.0 / math.sqrt(HEAD_DIM)
    holders, _, _, piece, _ = kv_ref.shape
    depth = holders * piece
    in_first = tok_slot_ref[...] == 0
    nt = (((1,), (1,)), ((), ()))
    tn = (((0,), (0,)), ((), ()))
    low = dkv_ref.dtype
    for head in range(HEADS_PER_STEP):
        cols = slice(head * HEAD_DIM, (head + 1) * HEAD_DIM)
        q = q_ref[:, cols]
        g = g_ref[:, cols]
        k0 = kv_ref[:, 0, 0, :, cols].reshape(depth, HEAD_DIM)
        k1 = kv_ref[:, 1, 0, :, cols].reshape(depth, HEAD_DIM)
        v0 = kv_ref[:, 0, 1, :, cols].reshape(depth, HEAD_DIM)
        v1 = kv_ref[:, 1, 1, :, cols].reshape(depth, HEAD_DIM)
        scores = jnp.where(
            in_first,
            lax.dot_general(q, k0, nt, preferred_element_type=jnp.float32),
            lax.dot_general(q, k1, nt, preferred_element_type=jnp.float32),
        ) * score_scale
        row_max = jnp.max(scores, axis=1, keepdims=True)
        weights = jnp.exp(scores - row_max)
        normed = weights * (1.0 / jnp.sum(weights, axis=1, keepdims=True))
        weights_low = normed.astype(jnp.bfloat16)
        attended = jnp.where(
            in_first,
            jnp.dot(weights_low, v0, preferred_element_type=jnp.float32),
            jnp.dot(weights_low, v1, preferred_element_type=jnp.float32),
        ).astype(jnp.bfloat16)
        delta = jnp.sum(g.astype(jnp.float32) * attended.astype(jnp.float32), axis=1, keepdims=True)
        grad_weights = jnp.where(
            in_first,
            lax.dot_general(g, v0, nt, preferred_element_type=jnp.float32),
            lax.dot_general(g, v1, nt, preferred_element_type=jnp.float32),
        )
        grad_scores = (normed * (grad_weights - delta) * score_scale).astype(jnp.bfloat16)
        dq_ref[:, cols] = jnp.where(
            in_first,
            jnp.dot(grad_scores, k0, preferred_element_type=jnp.float32),
            jnp.dot(grad_scores, k1, preferred_element_type=jnp.float32),
        ).astype(dq_ref.dtype)
        zero = jnp.zeros_like(grad_scores)
        gs0 = jnp.where(in_first, grad_scores, zero)
        gs1 = jnp.where(in_first, zero, grad_scores)
        w0 = jnp.where(in_first, weights_low, zero)
        w1 = jnp.where(in_first, zero, weights_low)
        for slot, (gs, w) in enumerate(((gs0, w0), (gs1, w1))):
            dk = lax.dot_general(gs, q, tn, preferred_element_type=jnp.float32).astype(low)
            dv = lax.dot_general(w, g, tn, preferred_element_type=jnp.float32).astype(low)
            dkv_ref[:, slot, 0, :, cols] = dk.reshape(holders, piece, HEAD_DIM)
            dkv_ref[:, slot, 1, :, cols] = dv.reshape(holders, piece, HEAD_DIM)


def attend(tok_slot, query_normed, kv, grad_out):
    tok_rows, feat_width = query_normed.shape
    step_width = HEADS_PER_STEP * HEAD_DIM
    tok_spec = pl.BlockSpec((tok_rows, step_width), lambda h: (0, h))
    kv_spec = pl.BlockSpec(kv.shape[:4] + (step_width,), lambda h: (0, 0, 0, 0, h))
    return pl.pallas_call(
        attend_kernel,
        grid=(feat_width // step_width,),
        in_specs=[
            pl.BlockSpec((tok_rows, 1), lambda h: (0, 0)),
            tok_spec,
            kv_spec,
            tok_spec,
        ],
        out_specs=[tok_spec, kv_spec],
        out_shape=[
            jax.ShapeDtypeStruct((tok_rows, feat_width), jnp.bfloat16),
            jax.ShapeDtypeStruct(kv.shape, jnp.bfloat16),
        ],
        compiler_params=pltpu.CompilerParams(dimension_semantics=("arbitrary",)),
    )(tok_slot, query_normed, kv, grad_out)


def local(query, query_gain, cond, key_gain, grad_out, clip_len, clip_owner, seq_count):
    tok_rows, feat_width = query.shape
    clip_count = clip_len.shape[0]
    cond_depth = cond.shape[2]
    piece = cond_depth // seq_count
    my_index = lax.axis_index("seq")
    first_pos = my_index * tok_rows
    position = first_pos + jnp.arange(tok_rows, dtype=jnp.int32)
    starts = jnp.cumsum(clip_len) - clip_len
    clip_of = jnp.sum((position[:, None] >= starts[None, :]).astype(jnp.int32), axis=1) - 1
    device_pos = jnp.arange(seq_count, dtype=jnp.int32) * tok_rows
    device_first = jnp.sum((device_pos[:, None] >= starts[None, :]).astype(jnp.int32), axis=1) - 1
    own_key = cond[0, 0].astype(jnp.float32)
    key_scale = lax.rsqrt(lax.psum(jnp.sum(own_key * own_key, axis=1), "mp") / D + EPS)
    own_key_normed = (own_key * key_scale[:, None] * key_gain).astype(jnp.bfloat16)
    own_slab = jnp.stack([own_key_normed, cond[0, 1]])
    spread = own_slab.reshape(2, seq_count, piece, feat_width)
    gathered = lax.all_to_all(spread, "seq", 1, 0, tiled=True).reshape(seq_count, 2, piece, feat_width)
    slot_clip = jnp.stack([device_first, device_first + 1], axis=1)
    wanted = jnp.take(gathered, clip_owner[jnp.minimum(slot_clip, clip_count - 1)], axis=0, mode="clip")
    arrived = lax.all_to_all(wanted, "seq", 0, 0, tiled=True)
    query_wide = query.astype(jnp.float32)
    after_first = (gathered[0, 0, 0, 0] * 0).astype(jnp.float32)
    query_sumsq = lax.psum(jnp.sum(query_wide * query_wide, axis=1) + after_first, "mp")
    query_scale = lax.rsqrt(query_sumsq / D + EPS)
    query_normed = (query_wide * query_scale[:, None] * query_gain).astype(jnp.bfloat16)
    tok_slot = clip_of - device_first[my_index]
    if piece % 16 == 0:
        grad_query, spread_grads = attend(tok_slot[:, None], query_normed, arrived, grad_out)
    else:
        mine = arrived.transpose(1, 2, 0, 3, 4).reshape(1, 2, 2, cond_depth, feat_width)
        grad_query, grad_slots = attend(tok_slot[:, None], query_normed, mine, grad_out)
        spread_grads = grad_slots[0].reshape(2, 2, seq_count, piece, feat_width).transpose(2, 0, 1, 3, 4)
    pieces = lax.all_to_all(spread_grads, "seq", 0, 0, tiled=True)
    source_clip = slot_clip.reshape(2 * seq_count)
    owns = clip_owner[None, :] == jnp.arange(seq_count, dtype=jnp.int32)[:, None]
    owned_clip = jnp.sum(jnp.where(owns, jnp.arange(clip_count, dtype=jnp.int32)[None, :], 0), axis=1)
    route = (source_clip[None, :] == owned_clip[:, None]) & jnp.any(owns, axis=1)[:, None]
    outgoing = jnp.einsum(
        "ds,sx->dx", route.astype(jnp.bfloat16), pieces.reshape(2 * seq_count, -1), preferred_element_type=jnp.float32
    ).astype(jnp.bfloat16).reshape(seq_count, 2, piece, feat_width)
    owned_grads = lax.all_to_all(outgoing, "seq", 0, 2, tiled=True).reshape(2, cond_depth, feat_width)
    return (grad_query, owned_grads[None])


def solution(mesh):
    seq_count = mesh.shape["seq"]

    def body(*args):
        return local(*args, seq_count)

    return jax.shard_map(
        body,
        mesh=mesh,
        in_specs=(
            P("seq", "mp"),
            P("mp"),
            P("seq", None, None, "mp"),
            P("mp"),
            P("seq", "mp"),
            P(),
            P(),
        ),
        out_specs=(P("seq", "mp"), P("seq", None, None, "mp")),
        check_vma=False,
    )
```

```python
import math

import jax
import jax.numpy as jnp
from jax import lax
from jax.experimental import pallas as pl
from jax.experimental.pallas import tpu as pltpu
from jax.sharding import PartitionSpec as P

D = 5120
HEAD_DIM = 128


EPS = 1e-06
MASKED = -1e30


HEADS_PER_STEP = 2


def attend_kernel(tok_slot_ref, q_ref, kv_ref, g_ref, dq_ref, dkv_ref):
    score_scale = 1.0 / math.sqrt(HEAD_DIM)
    holders, _, _, piece, _ = kv_ref.shape
    depth = holders * piece
    in_first = tok_slot_ref[...] == 0
    nt = (((1,), (1,)), ((), ()))
    tn = (((0,), (0,)), ((), ()))
    low = dkv_ref.dtype
    for head in range(HEADS_PER_STEP):
        cols = slice(head * HEAD_DIM, (head + 1) * HEAD_DIM)
        q = q_ref[:, cols]
        g = g_ref[:, cols]
        k0 = kv_ref[:, 0, 0, :, cols].reshape(depth, HEAD_DIM)
        k1 = kv_ref[:, 1, 0, :, cols].reshape(depth, HEAD_DIM)
        v0 = kv_ref[:, 0, 1, :, cols].reshape(depth, HEAD_DIM)
        v1 = kv_ref[:, 1, 1, :, cols].reshape(depth, HEAD_DIM)
        scores = jnp.where(
            in_first,
            lax.dot_general(q, k0, nt, preferred_element_type=jnp.float32),
            lax.dot_general(q, k1, nt, preferred_element_type=jnp.float32),
        ) * score_scale
        row_max = jnp.max(scores, axis=1, keepdims=True)
        weights = jnp.exp(scores - row_max)
        normed = weights * (1.0 / jnp.sum(weights, axis=1, keepdims=True))
        weights_low = normed.astype(jnp.bfloat16)
        attended = jnp.where(
            in_first,
            jnp.dot(weights_low, v0, preferred_element_type=jnp.float32),
            jnp.dot(weights_low, v1, preferred_element_type=jnp.float32),
        ).astype(jnp.bfloat16)
        delta = jnp.sum(g.astype(jnp.float32) * attended.astype(jnp.float32), axis=1, keepdims=True)
        grad_weights = jnp.where(
            in_first,
            lax.dot_general(g, v0, nt, preferred_element_type=jnp.float32),
            lax.dot_general(g, v1, nt, preferred_element_type=jnp.float32),
        )
        grad_scores = (normed * (grad_weights - delta) * score_scale).astype(jnp.bfloat16)
        dq_ref[:, cols] = jnp.where(
            in_first,
            jnp.dot(grad_scores, k0, preferred_element_type=jnp.float32),
            jnp.dot(grad_scores, k1, preferred_element_type=jnp.float32),
        ).astype(dq_ref.dtype)
        zero = jnp.zeros_like(grad_scores)
        gs0 = jnp.where(in_first, grad_scores, zero)
        gs1 = jnp.where(in_first, zero, grad_scores)
        w0 = jnp.where(in_first, weights_low, zero)
        w1 = jnp.where(in_first, zero, weights_low)
        for slot, (gs, w) in enumerate(((gs0, w0), (gs1, w1))):
            dk = lax.dot_general(gs, q, tn, preferred_element_type=jnp.float32).astype(low)
            dv = lax.dot_general(w, g, tn, preferred_element_type=jnp.float32).astype(low)
            dkv_ref[:, slot, 0, :, cols] = dk.reshape(holders, piece, HEAD_DIM)
            dkv_ref[:, slot, 1, :, cols] = dv.reshape(holders, piece, HEAD_DIM)


def attend(tok_slot, query_normed, kv, grad_out):
    tok_rows, feat_width = query_normed.shape
    step_width = HEADS_PER_STEP * HEAD_DIM
    tok_spec = pl.BlockSpec((tok_rows, step_width), lambda h: (0, h))
    kv_spec = pl.BlockSpec(kv.shape[:4] + (step_width,), lambda h: (0, 0, 0, 0, h))
    return pl.pallas_call(
        attend_kernel,
        grid=(feat_width // step_width,),
        in_specs=[
            pl.BlockSpec((tok_rows, 1), lambda h: (0, 0)),
            tok_spec,
            kv_spec,
            tok_spec,
        ],
        out_specs=[tok_spec, kv_spec],
        out_shape=[
            jax.ShapeDtypeStruct((tok_rows, feat_width), jnp.bfloat16),
            jax.ShapeDtypeStruct(kv.shape, jnp.bfloat16),
        ],
        compiler_params=pltpu.CompilerParams(dimension_semantics=("arbitrary",)),
    )(tok_slot, query_normed, kv, grad_out)


def local(query, query_gain, cond, key_gain, grad_out, clip_len, clip_owner, seq_count):
    tok_rows, feat_width = query.shape
    clip_count = clip_len.shape[0]
    cond_depth = cond.shape[2]
    piece = cond_depth // seq_count
    my_index = lax.axis_index("seq")
    first_pos = my_index * tok_rows
    position = first_pos + jnp.arange(tok_rows, dtype=jnp.int32)
    starts = jnp.cumsum(clip_len) - clip_len
    clip_of = jnp.sum((position[:, None] >= starts[None, :]).astype(jnp.int32), axis=1) - 1
    device_pos = jnp.arange(seq_count, dtype=jnp.int32) * tok_rows
    device_first = jnp.sum((device_pos[:, None] >= starts[None, :]).astype(jnp.int32), axis=1) - 1
    own_key = cond[0, 0].astype(jnp.float32)
    key_scale = lax.rsqrt(lax.psum(jnp.sum(own_key * own_key, axis=1), "mp") / D + EPS)
    own_key_normed = (own_key * key_scale[:, None] * key_gain).astype(jnp.bfloat16)
    own_slab = jnp.stack([own_key_normed, cond[0, 1]])
    spread = own_slab.reshape(2, seq_count, piece, feat_width)
    gathered = lax.all_to_all(spread, "seq", 1, 0, tiled=True).reshape(seq_count, 2, piece, feat_width)
    slot_clip = jnp.stack([device_first, device_first + 1], axis=1)
    source = clip_owner[jnp.minimum(slot_clip, clip_count - 1)]
    pick = (source[:, :, None] == jnp.arange(seq_count, dtype=jnp.int32)[None, None, :]).astype(jnp.bfloat16)
    wanted = jnp.einsum("dsn,nkrf->dskrf", pick, gathered, preferred_element_type=jnp.float32).astype(jnp.bfloat16)
    arrived = lax.all_to_all(wanted, "seq", 0, 0, tiled=True)
    query_wide = query.astype(jnp.float32)
    after_first = (gathered[0, 0, 0, 0] * 0).astype(jnp.float32)
    query_sumsq = lax.psum(jnp.sum(query_wide * query_wide, axis=1) + after_first, "mp")
    query_scale = lax.rsqrt(query_sumsq / D + EPS)
    query_normed = (query_wide * query_scale[:, None] * query_gain).astype(jnp.bfloat16)
    tok_slot = clip_of - device_first[my_index]
    if piece % 16 == 0:
        grad_query, spread_grads = attend(tok_slot[:, None], query_normed, arrived, grad_out)
    else:
        mine = arrived.transpose(1, 2, 0, 3, 4).reshape(1, 2, 2, cond_depth, feat_width)
        grad_query, grad_slots = attend(tok_slot[:, None], query_normed, mine, grad_out)
        spread_grads = grad_slots[0].reshape(2, 2, seq_count, piece, feat_width).transpose(2, 0, 1, 3, 4)
    pieces = lax.all_to_all(spread_grads, "seq", 0, 0, tiled=True)
    source_clip = slot_clip.reshape(2 * seq_count)
    owns = clip_owner[None, :] == jnp.arange(seq_count, dtype=jnp.int32)[:, None]
    owned_clip = jnp.sum(jnp.where(owns, jnp.arange(clip_count, dtype=jnp.int32)[None, :], 0), axis=1)
    route = (source_clip[None, :] == owned_clip[:, None]) & jnp.any(owns, axis=1)[:, None]
    route = route.astype(jnp.bfloat16).reshape(seq_count, seq_count, 2)
    outgoing = jnp.einsum(
        "dns,nskrf->dkrf", route, pieces, preferred_element_type=jnp.float32
    ).astype(jnp.bfloat16)
    owned_grads = lax.all_to_all(outgoing, "seq", 0, 2, tiled=True).reshape(2, cond_depth, feat_width)
    return (grad_query, owned_grads[None])


def solution(mesh):
    seq_count = mesh.shape["seq"]

    def body(*args):
        return local(*args, seq_count)

    return jax.shard_map(
        body,
        mesh=mesh,
        in_specs=(
            P("seq", "mp"),
            P("mp"),
            P("seq", None, None, "mp"),
            P("mp"),
            P("seq", "mp"),
            P(),
            P(),
        ),
        out_specs=(P("seq", "mp"), P("seq", None, None, "mp")),
        check_vma=False,
    )
```

```python
import math

import jax
import jax.numpy as jnp
from jax import lax
from jax.experimental import pallas as pl
from jax.experimental.pallas import tpu as pltpu
from jax.sharding import PartitionSpec as P

D = 5120
HEAD_DIM = 128


EPS = 1e-06
MASKED = -1e30


HEADS_PER_STEP = 2


def attend_kernel(tok_slot_ref, q_ref, kv_ref, g_ref, dq_ref, dkv_ref):
    score_scale = 1.0 / math.sqrt(HEAD_DIM)
    holders, _, _, piece, _ = kv_ref.shape
    depth = holders * piece
    in_first = tok_slot_ref[...] == 0
    nt = (((1,), (1,)), ((), ()))
    tn = (((0,), (0,)), ((), ()))
    low = dkv_ref.dtype
    for head in range(HEADS_PER_STEP):
        cols = slice(head * HEAD_DIM, (head + 1) * HEAD_DIM)
        q = q_ref[:, cols]
        g = g_ref[:, cols]
        k0 = kv_ref[:, 0, 0, :, cols].reshape(depth, HEAD_DIM)
        k1 = kv_ref[:, 1, 0, :, cols].reshape(depth, HEAD_DIM)
        v0 = kv_ref[:, 0, 1, :, cols].reshape(depth, HEAD_DIM)
        v1 = kv_ref[:, 1, 1, :, cols].reshape(depth, HEAD_DIM)
        scores = jnp.where(
            in_first,
            lax.dot_general(q, k0, nt, preferred_element_type=jnp.float32),
            lax.dot_general(q, k1, nt, preferred_element_type=jnp.float32),
        ) * score_scale
        row_max = jnp.max(scores, axis=1, keepdims=True)
        weights = jnp.exp(scores - row_max)
        normed = weights * (1.0 / jnp.sum(weights, axis=1, keepdims=True))
        weights_low = normed.astype(jnp.bfloat16)
        attended = jnp.where(
            in_first,
            jnp.dot(weights_low, v0, preferred_element_type=jnp.float32),
            jnp.dot(weights_low, v1, preferred_element_type=jnp.float32),
        ).astype(jnp.bfloat16)
        delta = jnp.sum(g.astype(jnp.float32) * attended.astype(jnp.float32), axis=1, keepdims=True)
        grad_weights = jnp.where(
            in_first,
            lax.dot_general(g, v0, nt, preferred_element_type=jnp.float32),
            lax.dot_general(g, v1, nt, preferred_element_type=jnp.float32),
        )
        grad_scores = (normed * (grad_weights - delta) * score_scale).astype(jnp.bfloat16)
        dq_ref[:, cols] = jnp.where(
            in_first,
            jnp.dot(grad_scores, k0, preferred_element_type=jnp.float32),
            jnp.dot(grad_scores, k1, preferred_element_type=jnp.float32),
        ).astype(dq_ref.dtype)
        zero = jnp.zeros_like(grad_scores)
        gs0 = jnp.where(in_first, grad_scores, zero)
        gs1 = jnp.where(in_first, zero, grad_scores)
        w0 = jnp.where(in_first, weights_low, zero)
        w1 = jnp.where(in_first, zero, weights_low)
        for slot, (gs, w) in enumerate(((gs0, w0), (gs1, w1))):
            dk = lax.dot_general(gs, q, tn, preferred_element_type=jnp.float32).astype(low)
            dv = lax.dot_general(w, g, tn, preferred_element_type=jnp.float32).astype(low)
            dkv_ref[:, slot, 0, :, cols] = dk.reshape(holders, piece, HEAD_DIM)
            dkv_ref[:, slot, 1, :, cols] = dv.reshape(holders, piece, HEAD_DIM)


def attend(tok_slot, query_normed, kv, grad_out):
    tok_rows, feat_width = query_normed.shape
    step_width = HEADS_PER_STEP * HEAD_DIM
    tok_spec = pl.BlockSpec((tok_rows, step_width), lambda h: (0, h))
    kv_spec = pl.BlockSpec(kv.shape[:4] + (step_width,), lambda h: (0, 0, 0, 0, h))
    return pl.pallas_call(
        attend_kernel,
        grid=(feat_width // step_width,),
        in_specs=[
            pl.BlockSpec((tok_rows, 1), lambda h: (0, 0)),
            tok_spec,
            kv_spec,
            tok_spec,
        ],
        out_specs=[tok_spec, kv_spec],
        out_shape=[
            jax.ShapeDtypeStruct((tok_rows, feat_width), jnp.bfloat16),
            jax.ShapeDtypeStruct(kv.shape, jnp.bfloat16),
        ],
        compiler_params=pltpu.CompilerParams(dimension_semantics=("arbitrary",)),
    )(tok_slot, query_normed, kv, grad_out)


def local(query, query_gain, cond, key_gain, grad_out, clip_len, clip_owner, seq_count):
    tok_rows, feat_width = query.shape
    clip_count = clip_len.shape[0]
    cond_depth = cond.shape[2]
    piece = cond_depth // seq_count
    my_index = lax.axis_index("seq")
    first_pos = my_index * tok_rows
    position = first_pos + jnp.arange(tok_rows, dtype=jnp.int32)
    starts = jnp.cumsum(clip_len) - clip_len
    clip_of = jnp.sum((position[:, None] >= starts[None, :]).astype(jnp.int32), axis=1) - 1
    device_pos = jnp.arange(seq_count, dtype=jnp.int32) * tok_rows
    device_first = jnp.sum((device_pos[:, None] >= starts[None, :]).astype(jnp.int32), axis=1) - 1
    own_key = cond[0, 0]
    key_sumsq = jnp.einsum("rf,rf->r", own_key, own_key, preferred_element_type=jnp.float32)
    key_scale = lax.rsqrt(lax.psum(key_sumsq, "mp") / D + EPS)
    own_key_normed = (own_key.astype(jnp.float32) * key_scale[:, None] * key_gain).astype(jnp.bfloat16)
    own_slab = jnp.stack([own_key_normed, cond[0, 1]])
    spread = own_slab.reshape(2, seq_count, piece, feat_width)
    gathered = lax.all_to_all(spread, "seq", 1, 0, tiled=True).reshape(seq_count, 2, piece, feat_width)
    slot_clip = jnp.stack([device_first, device_first + 1], axis=1)
    wanted = jnp.take(gathered, clip_owner[jnp.minimum(slot_clip, clip_count - 1)], axis=0, mode="clip")
    arrived = lax.all_to_all(wanted, "seq", 0, 0, tiled=True)
    query_wide = query.astype(jnp.float32)
    after_first = (gathered[0, 0, 0, 0] * 0).astype(jnp.float32)
    query_sumsq = lax.psum(jnp.sum(query_wide * query_wide, axis=1) + after_first, "mp")
    query_scale = lax.rsqrt(query_sumsq / D + EPS)
    query_normed = (query_wide * query_scale[:, None] * query_gain).astype(jnp.bfloat16)
    tok_slot = clip_of - device_first[my_index]
    if piece % 16 == 0:
        grad_query, spread_grads = attend(tok_slot[:, None], query_normed, arrived, grad_out)
    else:
        mine = arrived.transpose(1, 2, 0, 3, 4).reshape(1, 2, 2, cond_depth, feat_width)
        grad_query, grad_slots = attend(tok_slot[:, None], query_normed, mine, grad_out)
        spread_grads = grad_slots[0].reshape(2, 2, seq_count, piece, feat_width).transpose(2, 0, 1, 3, 4)
    pieces = lax.all_to_all(spread_grads, "seq", 0, 0, tiled=True)
    source_clip = slot_clip.reshape(2 * seq_count)
    owns = clip_owner[None, :] == jnp.arange(seq_count, dtype=jnp.int32)[:, None]
    owned_clip = jnp.sum(jnp.where(owns, jnp.arange(clip_count, dtype=jnp.int32)[None, :], 0), axis=1)
    route = (source_clip[None, :] == owned_clip[:, None]) & jnp.any(owns, axis=1)[:, None]
    outgoing = jnp.einsum(
        "ds,sx->dx", route.astype(jnp.bfloat16), pieces.reshape(2 * seq_count, -1), preferred_element_type=jnp.float32
    ).astype(jnp.bfloat16).reshape(seq_count, 2, piece, feat_width)
    owned_grads = lax.all_to_all(outgoing, "seq", 0, 2, tiled=True).reshape(2, cond_depth, feat_width)
    return (grad_query, owned_grads[None])


def solution(mesh):
    seq_count = mesh.shape["seq"]

    def body(*args):
        return local(*args, seq_count)

    return jax.shard_map(
        body,
        mesh=mesh,
        in_specs=(
            P("seq", "mp"),
            P("mp"),
            P("seq", None, None, "mp"),
            P("mp"),
            P("seq", "mp"),
            P(),
            P(),
        ),
        out_specs=(P("seq", "mp"), P("seq", None, None, "mp")),
        check_vma=False,
    )
```

```python
import math

import jax
import jax.numpy as jnp
from jax import lax
from jax.experimental import pallas as pl
from jax.experimental.pallas import tpu as pltpu
from jax.sharding import PartitionSpec as P

D = 5120
HEAD_DIM = 128


EPS = 1e-06
MASKED = -1e30


HEADS_PER_STEP = 2


def attend_kernel(tok_slot_ref, q_ref, kv_ref, g_ref, dq_ref, dkv_ref):
    score_scale = 1.0 / math.sqrt(HEAD_DIM)
    holders, _, _, piece, _ = kv_ref.shape
    depth = holders * piece
    in_first = tok_slot_ref[...] == 0
    nt = (((1,), (1,)), ((), ()))
    tn = (((0,), (0,)), ((), ()))
    low = dkv_ref.dtype
    for head in range(HEADS_PER_STEP):
        cols = slice(head * HEAD_DIM, (head + 1) * HEAD_DIM)
        q = q_ref[:, cols]
        g = g_ref[:, cols]
        k0 = kv_ref[:, 0, 0, :, cols].reshape(depth, HEAD_DIM)
        k1 = kv_ref[:, 1, 0, :, cols].reshape(depth, HEAD_DIM)
        v0 = kv_ref[:, 0, 1, :, cols].reshape(depth, HEAD_DIM)
        v1 = kv_ref[:, 1, 1, :, cols].reshape(depth, HEAD_DIM)
        scores = jnp.where(
            in_first,
            lax.dot_general(q, k0, nt, preferred_element_type=jnp.float32),
            lax.dot_general(q, k1, nt, preferred_element_type=jnp.float32),
        ) * score_scale
        row_max = jnp.max(scores, axis=1, keepdims=True)
        weights = jnp.exp(scores - row_max)
        normed = weights * (1.0 / jnp.sum(weights, axis=1, keepdims=True))
        weights_low = normed.astype(jnp.bfloat16)
        attended = jnp.where(
            in_first,
            jnp.dot(weights_low, v0, preferred_element_type=jnp.float32),
            jnp.dot(weights_low, v1, preferred_element_type=jnp.float32),
        ).astype(jnp.bfloat16)
        delta = jnp.sum(g.astype(jnp.float32) * attended.astype(jnp.float32), axis=1, keepdims=True)
        grad_weights = jnp.where(
            in_first,
            lax.dot_general(g, v0, nt, preferred_element_type=jnp.float32),
            lax.dot_general(g, v1, nt, preferred_element_type=jnp.float32),
        )
        grad_scores = (normed * (grad_weights - delta) * score_scale).astype(jnp.bfloat16)
        dq_ref[:, cols] = jnp.where(
            in_first,
            jnp.dot(grad_scores, k0, preferred_element_type=jnp.float32),
            jnp.dot(grad_scores, k1, preferred_element_type=jnp.float32),
        ).astype(dq_ref.dtype)
        zero = jnp.zeros_like(grad_scores)
        gs0 = jnp.where(in_first, grad_scores, zero)
        gs1 = jnp.where(in_first, zero, grad_scores)
        w0 = jnp.where(in_first, weights_low, zero)
        w1 = jnp.where(in_first, zero, weights_low)
        for slot, (gs, w) in enumerate(((gs0, w0), (gs1, w1))):
            dk = lax.dot_general(gs, q, tn, preferred_element_type=jnp.float32).astype(low)
            dv = lax.dot_general(w, g, tn, preferred_element_type=jnp.float32).astype(low)
            dkv_ref[:, slot, 0, :, cols] = dk.reshape(holders, piece, HEAD_DIM)
            dkv_ref[:, slot, 1, :, cols] = dv.reshape(holders, piece, HEAD_DIM)


def attend(tok_slot, query_normed, kv, grad_out):
    tok_rows, feat_width = query_normed.shape
    step_width = HEADS_PER_STEP * HEAD_DIM
    tok_spec = pl.BlockSpec((tok_rows, step_width), lambda h: (0, h))
    kv_spec = pl.BlockSpec(kv.shape[:4] + (step_width,), lambda h: (0, 0, 0, 0, h))
    return pl.pallas_call(
        attend_kernel,
        grid=(feat_width // step_width,),
        in_specs=[
            pl.BlockSpec((tok_rows, 1), lambda h: (0, 0)),
            tok_spec,
            kv_spec,
            tok_spec,
        ],
        out_specs=[tok_spec, kv_spec],
        out_shape=[
            jax.ShapeDtypeStruct((tok_rows, feat_width), jnp.bfloat16),
            jax.ShapeDtypeStruct(kv.shape, jnp.bfloat16),
        ],
        compiler_params=pltpu.CompilerParams(dimension_semantics=("arbitrary",)),
    )(tok_slot, query_normed, kv, grad_out)


def local(query, query_gain, cond, key_gain, grad_out, clip_len, clip_owner, seq_count):
    tok_rows, feat_width = query.shape
    clip_count = clip_len.shape[0]
    cond_depth = cond.shape[2]
    piece = cond_depth // seq_count
    my_index = lax.axis_index("seq")
    first_pos = my_index * tok_rows
    position = first_pos + jnp.arange(tok_rows, dtype=jnp.int32)
    starts = jnp.cumsum(clip_len) - clip_len
    clip_of = jnp.sum((position[:, None] >= starts[None, :]).astype(jnp.int32), axis=1) - 1
    device_pos = jnp.arange(seq_count, dtype=jnp.int32) * tok_rows
    device_first = jnp.sum((device_pos[:, None] >= starts[None, :]).astype(jnp.int32), axis=1) - 1
    own_key = cond[0, 0].astype(jnp.float32)
    key_scale = lax.rsqrt(lax.psum(jnp.sum(own_key * own_key, axis=1), "mp") / D + EPS)
    own_key_normed = (own_key * key_scale[:, None] * key_gain).astype(jnp.bfloat16)
    own_slab = jnp.stack([own_key_normed, cond[0, 1]])
    spread = own_slab.reshape(2, seq_count, piece, feat_width)
    gathered = lax.all_to_all(spread, "seq", 1, 0, tiled=True).reshape(seq_count, 2, piece, feat_width)
    slot_clip = jnp.stack([device_first, device_first + 1], axis=1)
    owner_rows = jnp.take(gathered, clip_owner, axis=0, mode="clip")
    slot_of = slot_clip[:, :, None, None, None]
    wanted = owner_rows[clip_count - 1][None, None]
    for clip in range(clip_count - 2, -1, -1):
        wanted = jnp.where(slot_of == clip, owner_rows[clip][None, None], wanted)
    arrived = lax.all_to_all(wanted, "seq", 0, 0, tiled=True)
    query_wide = query.astype(jnp.float32)
    after_first = (gathered[0, 0, 0, 0] * 0).astype(jnp.float32)
    query_sumsq = lax.psum(jnp.sum(query_wide * query_wide, axis=1) + after_first, "mp")
    query_scale = lax.rsqrt(query_sumsq / D + EPS)
    query_normed = (query_wide * query_scale[:, None] * query_gain).astype(jnp.bfloat16)
    tok_slot = clip_of - device_first[my_index]
    if piece % 16 == 0:
        grad_query, spread_grads = attend(tok_slot[:, None], query_normed, arrived, grad_out)
    else:
        mine = arrived.transpose(1, 2, 0, 3, 4).reshape(1, 2, 2, cond_depth, feat_width)
        grad_query, grad_slots = attend(tok_slot[:, None], query_normed, mine, grad_out)
        spread_grads = grad_slots[0].reshape(2, 2, seq_count, piece, feat_width).transpose(2, 0, 1, 3, 4)
    pieces = lax.all_to_all(spread_grads, "seq", 0, 0, tiled=True)
    source_clip = slot_clip.reshape(2 * seq_count)
    owns = clip_owner[None, :] == jnp.arange(seq_count, dtype=jnp.int32)[:, None]
    owned_clip = jnp.sum(jnp.where(owns, jnp.arange(clip_count, dtype=jnp.int32)[None, :], 0), axis=1)
    route = (source_clip[None, :] == owned_clip[:, None]) & jnp.any(owns, axis=1)[:, None]
    outgoing = jnp.einsum(
        "ds,sx->dx", route.astype(jnp.bfloat16), pieces.reshape(2 * seq_count, -1), preferred_element_type=jnp.float32
    ).astype(jnp.bfloat16).reshape(seq_count, 2, piece, feat_width)
    owned_grads = lax.all_to_all(outgoing, "seq", 0, 2, tiled=True).reshape(2, cond_depth, feat_width)
    return (grad_query, owned_grads[None])


def solution(mesh):
    seq_count = mesh.shape["seq"]

    def body(*args):
        return local(*args, seq_count)

    return jax.shard_map(
        body,
        mesh=mesh,
        in_specs=(
            P("seq", "mp"),
            P("mp"),
            P("seq", None, None, "mp"),
            P("mp"),
            P("seq", "mp"),
            P(),
            P(),
        ),
        out_specs=(P("seq", "mp"), P("seq", None, None, "mp")),
        check_vma=False,
    )
```

```python
import math

import jax
import jax.numpy as jnp
from jax import lax
from jax.experimental import pallas as pl
from jax.experimental.pallas import tpu as pltpu
from jax.sharding import PartitionSpec as P

D = 5120
HEAD_DIM = 128


EPS = 1e-06
MASKED = -1e30


HEADS_PER_STEP = 5


def attend_kernel(tok_slot_ref, q_ref, kv_ref, g_ref, dq_ref, dkv_ref):
    score_scale = 1.0 / math.sqrt(HEAD_DIM)
    holders, _, _, piece, _ = kv_ref.shape
    depth = holders * piece
    in_first = tok_slot_ref[...] == 0
    nt = (((1,), (1,)), ((), ()))
    tn = (((0,), (0,)), ((), ()))
    low = dkv_ref.dtype
    for head in range(HEADS_PER_STEP):
        cols = slice(head * HEAD_DIM, (head + 1) * HEAD_DIM)
        q = q_ref[:, cols]
        g = g_ref[:, cols]
        k0 = kv_ref[:, 0, 0, :, cols].reshape(depth, HEAD_DIM)
        k1 = kv_ref[:, 1, 0, :, cols].reshape(depth, HEAD_DIM)
        v0 = kv_ref[:, 0, 1, :, cols].reshape(depth, HEAD_DIM)
        v1 = kv_ref[:, 1, 1, :, cols].reshape(depth, HEAD_DIM)
        scores = jnp.where(
            in_first,
            lax.dot_general(q, k0, nt, preferred_element_type=jnp.float32),
            lax.dot_general(q, k1, nt, preferred_element_type=jnp.float32),
        ) * score_scale
        row_max = jnp.max(scores, axis=1, keepdims=True)
        weights = jnp.exp(scores - row_max)
        normed = weights * (1.0 / jnp.sum(weights, axis=1, keepdims=True))
        weights_low = normed.astype(jnp.bfloat16)
        attended = jnp.where(
            in_first,
            jnp.dot(weights_low, v0, preferred_element_type=jnp.float32),
            jnp.dot(weights_low, v1, preferred_element_type=jnp.float32),
        ).astype(jnp.bfloat16)
        delta = jnp.sum(g.astype(jnp.float32) * attended.astype(jnp.float32), axis=1, keepdims=True)
        grad_weights = jnp.where(
            in_first,
            lax.dot_general(g, v0, nt, preferred_element_type=jnp.float32),
            lax.dot_general(g, v1, nt, preferred_element_type=jnp.float32),
        )
        grad_scores = (normed * (grad_weights - delta) * score_scale).astype(jnp.bfloat16)
        dq_ref[:, cols] = jnp.where(
            in_first,
            jnp.dot(grad_scores, k0, preferred_element_type=jnp.float32),
            jnp.dot(grad_scores, k1, preferred_element_type=jnp.float32),
        ).astype(dq_ref.dtype)
        zero = jnp.zeros_like(grad_scores)
        gs0 = jnp.where(in_first, grad_scores, zero)
        gs1 = jnp.where(in_first, zero, grad_scores)
        w0 = jnp.where(in_first, weights_low, zero)
        w1 = jnp.where(in_first, zero, weights_low)
        for slot, (gs, w) in enumerate(((gs0, w0), (gs1, w1))):
            dk = lax.dot_general(gs, q, tn, preferred_element_type=jnp.float32).astype(low)
            dv = lax.dot_general(w, g, tn, preferred_element_type=jnp.float32).astype(low)
            dkv_ref[:, slot, 0, :, cols] = dk.reshape(holders, piece, HEAD_DIM)
            dkv_ref[:, slot, 1, :, cols] = dv.reshape(holders, piece, HEAD_DIM)


def attend(tok_slot, query_normed, kv, grad_out):
    tok_rows, feat_width = query_normed.shape
    step_width = HEADS_PER_STEP * HEAD_DIM
    tok_spec = pl.BlockSpec((tok_rows, step_width), lambda h: (0, h))
    kv_spec = pl.BlockSpec(kv.shape[:4] + (step_width,), lambda h: (0, 0, 0, 0, h))
    return pl.pallas_call(
        attend_kernel,
        grid=(feat_width // step_width,),
        in_specs=[
            pl.BlockSpec((tok_rows, 1), lambda h: (0, 0)),
            tok_spec,
            kv_spec,
            tok_spec,
        ],
        out_specs=[tok_spec, kv_spec],
        out_shape=[
            jax.ShapeDtypeStruct((tok_rows, feat_width), jnp.bfloat16),
            jax.ShapeDtypeStruct(kv.shape, jnp.bfloat16),
        ],
        compiler_params=pltpu.CompilerParams(dimension_semantics=("arbitrary",)),
    )(tok_slot, query_normed, kv, grad_out)


def local(query, query_gain, cond, key_gain, grad_out, clip_len, clip_owner, seq_count):
    tok_rows, feat_width = query.shape
    clip_count = clip_len.shape[0]
    cond_depth = cond.shape[2]
    piece = cond_depth // seq_count
    my_index = lax.axis_index("seq")
    first_pos = my_index * tok_rows
    position = first_pos + jnp.arange(tok_rows, dtype=jnp.int32)
    starts = jnp.cumsum(clip_len) - clip_len
    clip_of = jnp.sum((position[:, None] >= starts[None, :]).astype(jnp.int32), axis=1) - 1
    device_pos = jnp.arange(seq_count, dtype=jnp.int32) * tok_rows
    device_first = jnp.sum((device_pos[:, None] >= starts[None, :]).astype(jnp.int32), axis=1) - 1
    own_key = cond[0, 0].astype(jnp.float32)
    key_scale = lax.rsqrt(lax.psum(jnp.sum(own_key * own_key, axis=1), "mp") / D + EPS)
    own_key_normed = (own_key * key_scale[:, None] * key_gain).astype(jnp.bfloat16)
    own_slab = jnp.stack([own_key_normed, cond[0, 1]])
    spread = own_slab.reshape(2, seq_count, piece, feat_width)
    gathered = lax.all_to_all(spread, "seq", 1, 0, tiled=True).reshape(seq_count, 2, piece, feat_width)
    slot_clip = jnp.stack([device_first, device_first + 1], axis=1)
    wanted = jnp.take(gathered, clip_owner[jnp.minimum(slot_clip, clip_count - 1)], axis=0, mode="clip")
    arrived = lax.all_to_all(wanted, "seq", 0, 0, tiled=True)
    query_wide = query.astype(jnp.float32)
    after_first = (gathered[0, 0, 0, 0] * 0).astype(jnp.float32)
    query_sumsq = lax.psum(jnp.sum(query_wide * query_wide, axis=1) + after_first, "mp")
    query_scale = lax.rsqrt(query_sumsq / D + EPS)
    query_normed = (query_wide * query_scale[:, None] * query_gain).astype(jnp.bfloat16)
    tok_slot = clip_of - device_first[my_index]
    if piece % 16 == 0:
        grad_query, spread_grads = attend(tok_slot[:, None], query_normed, arrived, grad_out)
    else:
        mine = arrived.transpose(1, 2, 0, 3, 4).reshape(1, 2, 2, cond_depth, feat_width)
        grad_query, grad_slots = attend(tok_slot[:, None], query_normed, mine, grad_out)
        spread_grads = grad_slots[0].reshape(2, 2, seq_count, piece, feat_width).transpose(2, 0, 1, 3, 4)
    pieces = lax.all_to_all(spread_grads, "seq", 0, 0, tiled=True)
    source_clip = slot_clip.reshape(2 * seq_count)
    owns = clip_owner[None, :] == jnp.arange(seq_count, dtype=jnp.int32)[:, None]
    owned_clip = jnp.sum(jnp.where(owns, jnp.arange(clip_count, dtype=jnp.int32)[None, :], 0), axis=1)
    route = (source_clip[None, :] == owned_clip[:, None]) & jnp.any(owns, axis=1)[:, None]
    outgoing = jnp.einsum(
        "ds,sx->dx", route.astype(jnp.bfloat16), pieces.reshape(2 * seq_count, -1), preferred_element_type=jnp.float32
    ).astype(jnp.bfloat16).reshape(seq_count, 2, piece, feat_width)
    owned_grads = lax.all_to_all(outgoing, "seq", 0, 2, tiled=True).reshape(2, cond_depth, feat_width)
    return (grad_query, owned_grads[None])


def solution(mesh):
    seq_count = mesh.shape["seq"]

    def body(*args):
        return local(*args, seq_count)

    return jax.shard_map(
        body,
        mesh=mesh,
        in_specs=(
            P("seq", "mp"),
            P("mp"),
            P("seq", None, None, "mp"),
            P("mp"),
            P("seq", "mp"),
            P(),
            P(),
        ),
        out_specs=(P("seq", "mp"), P("seq", None, None, "mp")),
        check_vma=False,
    )
```
